128 devices in a mesh: slab: 8 (over z_lo, x), tile: 16 (over y, z_hi, core).
Axes of the slice: x: 4, y: 4, z: 4 (z_hi: 2, z_lo: 2; z = z_hi * 2 + z_lo), core: 2. Of those that a mesh axis runs over, the one named last changes fastest.
Arguments:
- base_flow: float32 [2, 64, 1024, 128], P(None, 'slab', 'tile'), may hold values from -0.4 to 0.8
- forcing: float32 [64, 4, 1024, 128], P('slab', None, 'tile'), may hold values from -6 to 6
- damping: float32 [1024, 128], P('tile'), may hold values from 0.005 to 0.2
- harmonics: int32 [8], replicated, may hold values from 1 to 31, as said below
Outputs:
- sketch: float32 [8, 2, 4, 1024, 128], P('slab', None, None, 'tile')
The draws below stay inside these ranges and needn't reach their ends.
Inputs may be any that keep to these rules, and one draw needn't show every extreme that they name: `harmonics`: distinct harmonic indices.
All inputs are finite; a program needn't handle non-finite values.
Results may differ from the reference program's by a relative error of at most 0.0003.
Values sent between devices are 32-bit elements; how exact they have to be, the bound alone decides.
No kernel may reach another device: no remote copies, remote signals or barrier semaphores. Data moves between devices by JAX's collectives and lax.ppermute only.
A program may use at most 64 MiB of HBM per device.

```python
import math
import jax
import jax.numpy as jnp
from jax import lax

NY = 128
STEPS = 8
SWEEPS = 2
NF = 4
H = 8
PHASES = 64
NX = 1024


def draw_harmonics(key, part):
    chosen = jax.random.permutation(key, PHASES // 2 - 1)[:H] + 1
    return chosen.astype(jnp.int32)


def draw_base_flow(key, part):
    key_stream = jax.random.fold_in(key, 11)
    key_cross = jax.random.fold_in(key, 12)
    shape = (PHASES, NX, NY)
    stream = 0.4 * jnp.exp(jax.random.uniform(key_stream, shape, jnp.float32, 0.0, math.log(2.0)))
    stream = jnp.clip(stream, 0.4, 0.8)
    turn = jax.random.uniform(key_cross, shape, jnp.float32, -math.pi, math.pi)
    cross = jnp.clip(0.4 * jnp.sin(turn), -0.4, 0.4)
    return jnp.stack([stream, cross]).astype(jnp.float32)


def shard_levels(key, shape, cuts, smallest, high):
    level = 1.0
    for axis_at, parts in cuts:
        steps = jax.random.uniform(jax.random.fold_in(jax.random.fold_in(key, 6), axis_at), (parts,), jnp.float32, smallest / len(cuts), high / len(cuts))
        level = level * jnp.repeat(jnp.exp(steps), shape[axis_at] // parts).reshape((-1,) + (1,) * (len(shape) - 1 - axis_at))
    return level


def noise(own_key, shape, scale, limit, split=(), held_as=jnp.bfloat16):
    result = scale * jax.random.normal(own_key, shape, jnp.float32)
    if split:
        result = result * shard_levels(own_key, shape, split, -0.22, 0.18)
    return jnp.clip(result, -limit, limit).astype(held_as)


def setup_inputs(seed: int = 0) -> dict:
    seeds = jax.random.split(jax.random.key(seed), 5)
    return {
        "base_flow": draw_base_flow(jax.random.fold_in(seeds[4], 71), 0),
        "forcing": noise(seeds[1], (PHASES, NF, NX, NY), 1.0, 6.0, ((0, 8), (2, 16)), jnp.float32),
        "damping": jnp.clip(jnp.exp(math.log(0.2) - 3.6888795 * jax.random.uniform(seeds[2], (NX, NY), jnp.float32) ** shard_levels(seeds[2], (NX, NY), ((0, 16),), -0.2, 0.2)), 0.005, 0.2),
        "harmonics": draw_harmonics(jax.random.fold_in(seeds[4], 71), 0),
    }


DIFFUSE = 0.15

def pad_grid(field):
    widths = [(0, 0)] * (field.ndim - 2) + [(1, 1), (1, 1)]
    return jnp.pad(field, widths)

def laplace(padded, center):
    return padded[..., 2:, 1:-1] + padded[..., :-2, 1:-1] + padded[..., 1:-1, 2:] + padded[..., 1:-1, :-2] - 4.0 * center

def forward_rate(state, speed_x, speed_y, damping, source):
    padded = pad_grid(state)
    grad_x = 0.5 * (padded[..., 2:, 1:-1] - padded[..., :-2, 1:-1])
    grad_y = 0.5 * (padded[..., 1:-1, 2:] - padded[..., 1:-1, :-2])
    return source - (speed_x * grad_x + speed_y * grad_y) + DIFFUSE * laplace(padded, state) - damping * state

def adjoint_rate(state, speed_x, speed_y, damping, source):
    padded = pad_grid(state)
    flux_x = pad_grid(speed_x * state)
    flux_y = pad_grid(speed_y * state)
    div_x = 0.5 * (flux_x[..., 2:, 1:-1] - flux_x[..., :-2, 1:-1])
    div_y = 0.5 * (flux_y[..., 1:-1, 2:] - flux_y[..., 1:-1, :-2])
    return source + div_x + div_y + DIFFUSE * laplace(padded, state) - damping * state

def reference(base_flow, forcing, damping, harmonics):
    slabs = PHASES // STEPS
    flow = base_flow.reshape(2, slabs, STEPS, NX, NY)
    drive = forcing.reshape(slabs, STEPS, NF, NX, NY)
    start = jnp.zeros((slabs, NF, NX, NY), jnp.float32)
    for sweep in range(SWEEPS):
        state = start
        record = []
        for step in range(STEPS):
            record.append(state)
            speed_x = flow[0, :, step][:, None]
            speed_y = flow[1, :, step][:, None]
            first = forward_rate(state, speed_x, speed_y, damping, drive[:, step])
            second = forward_rate(state + first, speed_x, speed_y, damping, drive[:, step])
            state = state + 0.5 * (first + second)
        start = jnp.roll(state, 1, axis=0)
    response = jnp.stack(record, axis=1)
    start = jnp.zeros((slabs, NF, NX, NY), jnp.float32)
    for sweep in range(SWEEPS):
        state = start
        record = [None] * STEPS
        for step in range(STEPS - 1, -1, -1):
            speed_x = flow[0, :, step][:, None]
            speed_y = flow[1, :, step][:, None]
            first = adjoint_rate(state, speed_x, speed_y, damping, response[:, step])
            second = adjoint_rate(state + first, speed_x, speed_y, damping, response[:, step])
            state = state + 0.5 * (first + second)
            record[step] = state
        start = jnp.roll(state, -1, axis=0)
    adjoint = jnp.stack(record, axis=1).reshape(PHASES, NF * NX * NY)
    phase = jnp.arange(PHASES, dtype=jnp.int32)
    turns = harmonics[:, None] * phase[None, :] % PHASES
    angle = 2.0 * math.pi / PHASES * turns.astype(jnp.float32)
    table = jnp.stack([jnp.cos(angle), -jnp.sin(angle)], axis=1) * (1.0 / math.sqrt(PHASES))
    table = table.reshape(2 * H, PHASES)
    sketch = jnp.dot(table, adjoint, precision=lax.Precision.HIGHEST)
    return sketch.reshape(H, 2, NF, NX, NY)
```

```python
import math

import jax
import jax.numpy as jnp
from jax import lax
from jax.sharding import PartitionSpec as P

SWEEPS = 2
H = 8


DIFFUSE = 0.15


def passed_along(block, axis, distance):
    devices = range(lax.axis_size(axis))
    route = [((i - distance) % len(devices), i) for i in devices]
    return lax.ppermute(block, axis, route)


def with_neighbours(block, axis, dim):
    count = lax.axis_size(axis)
    before = lax.ppermute(block, axis, [(i, i + 1) for i in range(count - 1)])
    after = lax.ppermute(block, axis, [(i + 1, i) for i in range(count - 1)])
    return jnp.concatenate([before, block, after], axis=dim)


def pad_grid(field):
    widths = [(0, 0)] * (field.ndim - 2) + [(1, 1), (1, 1)]
    return jnp.pad(field, widths)


def laplace(padded, center):
    return (
        padded[..., 2:, 1:-1]
        + padded[..., :-2, 1:-1]
        + padded[..., 1:-1, 2:]
        + padded[..., 1:-1, :-2]
        - 4.0 * center
    )


def forward_rate(state, speed_x, speed_y, damping, source, mask):
    padded = pad_grid(state)
    grad_x = 0.5 * (padded[..., 2:, 1:-1] - padded[..., :-2, 1:-1])
    grad_y = 0.5 * (padded[..., 1:-1, 2:] - padded[..., 1:-1, :-2])
    rate = source - (speed_x * grad_x + speed_y * grad_y) + DIFFUSE * laplace(padded, state) - damping * state
    return rate * mask


def adjoint_rate(state, speed_x, speed_y, damping, source, mask):
    padded = pad_grid(state)
    flux_x = pad_grid(speed_x * state)
    flux_y = pad_grid(speed_y * state)
    div_x = 0.5 * (flux_x[..., 2:, 1:-1] - flux_x[..., :-2, 1:-1])
    div_y = 0.5 * (flux_y[..., 1:-1, 2:] - flux_y[..., 1:-1, :-2])
    rate = source + div_x + div_y + DIFFUSE * laplace(padded, state) - damping * state
    return rate * mask


def coefficient_table(chosen, phase, periods):
    turns = chosen[:, None] * phase[None, :] % periods
    angle = 2.0 * math.pi / periods * turns.astype(jnp.float32)
    table = jnp.stack([jnp.cos(angle), -jnp.sin(angle)], axis=1) * (1.0 / math.sqrt(periods))
    return table.reshape(2 * chosen.shape[0], phase.shape[0])


def on_device(base_flow, forcing, damping, harmonics):
    steps = forcing.shape[0]
    count_f, rows, columns = (forcing.shape[1], forcing.shape[2], forcing.shape[3])
    slabs = lax.axis_size("slab")
    tiles = lax.axis_size("tile")
    periods = steps * slabs

    packed = jnp.concatenate(
        [base_flow.reshape(2 * steps, rows, columns), forcing.reshape(steps * count_f, rows, columns), damping[None]],
        axis=0,
    )
    wide = with_neighbours(packed, "tile", 1)
    ext = 3 * rows
    flow = wide[: 2 * steps].reshape(2, steps, ext, columns)
    drive = wide[2 * steps : 2 * steps + steps * count_f].reshape(steps, count_f, ext, columns)
    damp = wide[-1]
    row = lax.axis_index("tile") * rows - rows + jnp.arange(ext, dtype=jnp.int32)
    mask = ((row >= 0) & (row < tiles * rows)).astype(jnp.float32)[:, None]

    start = jnp.zeros((count_f, ext, columns), jnp.float32)
    for sweep in range(SWEEPS):
        state = start
        record = []
        for step in range(steps):
            record.append(state)
            speed_x = flow[0, step]
            speed_y = flow[1, step]
            first = forward_rate(state, speed_x, speed_y, damp, drive[step], mask)
            second = forward_rate(state + first, speed_x, speed_y, damp, drive[step], mask)
            state = state + 0.5 * (first + second)
        if sweep + 1 < SWEEPS:
            start = passed_along(state, "slab", 1)
    response = record
    start = jnp.zeros((count_f, ext, columns), jnp.float32)
    for sweep in range(SWEEPS):
        state = start
        record = [None] * steps
        for step in range(steps - 1, -1, -1):
            speed_x = flow[0, step]
            speed_y = flow[1, step]
            first = adjoint_rate(state, speed_x, speed_y, damp, response[step], mask)
            second = adjoint_rate(state + first, speed_x, speed_y, damp, response[step], mask)
            state = state + 0.5 * (first + second)
            record[step] = state
        if sweep + 1 < SWEEPS:
            start = passed_along(state, "slab", -1)
    adjoint = jnp.stack(record, axis=0)[:, :, rows : 2 * rows]
    phase = lax.axis_index("slab") * steps + jnp.arange(steps, dtype=jnp.int32)
    flat = adjoint.reshape(steps, count_f * rows * columns)
    table = coefficient_table(harmonics, phase, periods)
    terms = jnp.dot(table, flat, precision=lax.Precision.HIGHEST)
    return lax.psum_scatter(
        terms.reshape(H // slabs * lax.axis_size("slab"), 2, count_f, rows, columns),
        "slab",
        scatter_dimension=0,
        tiled=True,
    )


def solution(mesh):
    return jax.shard_map(
        on_device,
        mesh=mesh,
        in_specs=(
            P(None, "slab", "tile", None),
            P("slab", None, "tile", None),
            P("tile", None),
            P(),
        ),
        out_specs=P("slab", None, None, "tile", None),
        check_vma=False,
    )
```

```python
import math

import jax
import jax.numpy as jnp
from jax import lax
from jax.sharding import PartitionSpec as P

SWEEPS = 2
H = 8


DIFFUSE = 0.15


def passed_along(block, axis, distance):
    devices = range(lax.axis_size(axis))
    route = [((i - distance) % len(devices), i) for i in devices]
    return lax.ppermute(block, axis, route)


def with_neighbours(block, axis, dim):
    count = lax.axis_size(axis)
    before = lax.ppermute(block, axis, [(i, i + 1) for i in range(count - 1)])
    after = lax.ppermute(block, axis, [(i + 1, i) for i in range(count - 1)])
    return jnp.concatenate([before, block, after], axis=dim)


def pad_grid(field):
    widths = [(0, 0)] * (field.ndim - 2) + [(1, 1), (1, 1)]
    return jnp.pad(field, widths)


def laplace(padded, center):
    return (
        padded[..., 2:, 1:-1]
        + padded[..., :-2, 1:-1]
        + padded[..., 1:-1, 2:]
        + padded[..., 1:-1, :-2]
        - 4.0 * center
    )


def forward_rate(state, speed_x, speed_y, damping, source, mask):
    padded = pad_grid(state)
    grad_x = 0.5 * (padded[..., 2:, 1:-1] - padded[..., :-2, 1:-1])
    grad_y = 0.5 * (padded[..., 1:-1, 2:] - padded[..., 1:-1, :-2])
    rate = source - (speed_x * grad_x + speed_y * grad_y) + DIFFUSE * laplace(padded, state) - damping * state
    return rate * mask


def adjoint_rate(state, speed_x, speed_y, damping, source, mask):
    padded = pad_grid(state)
    flux_x = pad_grid(speed_x * state)
    flux_y = pad_grid(speed_y * state)
    div_x = 0.5 * (flux_x[..., 2:, 1:-1] - flux_x[..., :-2, 1:-1])
    div_y = 0.5 * (flux_y[..., 1:-1, 2:] - flux_y[..., 1:-1, :-2])
    rate = source + div_x + div_y + DIFFUSE * laplace(padded, state) - damping * state
    return rate * mask


def coefficient_table(chosen, phase, periods):
    turns = chosen[:, None] * phase[None, :] % periods
    angle = 2.0 * math.pi / periods * turns.astype(jnp.float32)
    table = jnp.stack([jnp.cos(angle), -jnp.sin(angle)], axis=1) * (1.0 / math.sqrt(periods))
    return table.reshape(2 * chosen.shape[0], phase.shape[0])


def on_device(base_flow, forcing, damping, harmonics):
    steps = forcing.shape[0]
    count_f, rows, columns = (forcing.shape[1], forcing.shape[2], forcing.shape[3])
    slabs = lax.axis_size("slab")
    tiles = lax.axis_size("tile")
    periods = steps * slabs

    packed = jnp.concatenate(
        [base_flow.reshape(2 * steps, rows, columns), forcing.reshape(steps * count_f, rows, columns), damping[None]],
        axis=0,
    )
    wide = with_neighbours(packed, "tile", 1)
    ext = 3 * rows
    flow = wide[: 2 * steps].reshape(2, steps, ext, columns)
    drive = wide[2 * steps : 2 * steps + steps * count_f].reshape(steps, count_f, ext, columns)
    damp = wide[-1]
    row = lax.axis_index("tile") * rows - rows + jnp.arange(ext, dtype=jnp.int32)
    mask = ((row >= 0) & (row < tiles * rows)).astype(jnp.float32)[:, None]

    phase = lax.axis_index("slab") * steps + jnp.arange(steps, dtype=jnp.int32)
    table = coefficient_table(harmonics, phase, periods)
    pieces = []
    for chunk in range(count_f):
        pieces.append(one_forcing(flow, drive[:, chunk : chunk + 1], damp, mask, table, rows))
    return jnp.concatenate(pieces, axis=2)


def gathered_sum(terms, axis):
    count = lax.axis_size(axis)
    here = lax.axis_index(axis)
    total = lax.dynamic_slice_in_dim(terms, here, 1, 0)
    for distance in range(1, count):
        part = lax.dynamic_slice_in_dim(terms, (here + distance) % count, 1, 0)
        total = total + lax.ppermute(part, axis, [(i, (i + distance) % count) for i in range(count)])
    return total


def one_forcing(flow, drive, damp, mask, table, rows):
    steps = drive.shape[0]
    count_f, ext, columns = drive.shape[1:]
    start = jnp.zeros((count_f, ext, columns), jnp.float32)
    for sweep in range(SWEEPS):
        state = start
        record = []
        for step in range(steps):
            record.append(state)
            speed_x = flow[0, step]
            speed_y = flow[1, step]
            first = forward_rate(state, speed_x, speed_y, damp, drive[step], mask)
            second = forward_rate(state + first, speed_x, speed_y, damp, drive[step], mask)
            state = state + 0.5 * (first + second)
        if sweep + 1 < SWEEPS:
            start = passed_along(state, "slab", 1)
    response = record
    start = jnp.zeros((count_f, ext, columns), jnp.float32)
    for sweep in range(SWEEPS):
        state = start
        record = [None] * steps
        for step in range(steps - 1, -1, -1):
            speed_x = flow[0, step]
            speed_y = flow[1, step]
            first = adjoint_rate(state, speed_x, speed_y, damp, response[step], mask)
            second = adjoint_rate(state + first, speed_x, speed_y, damp, response[step], mask)
            state = state + 0.5 * (first + second)
            record[step] = state
        if sweep + 1 < SWEEPS:
            start = passed_along(state, "slab", -1)
    adjoint = jnp.stack(record, axis=0)[:, :, rows : 2 * rows]
    flat = adjoint.reshape(steps, count_f * rows * columns)
    terms = jnp.dot(table, flat, precision=lax.Precision.HIGHEST)
    slabs = lax.axis_size("slab")
    return gathered_sum(terms.reshape(slabs, table.shape[0] // slabs, count_f, rows, columns), "slab")


def solution(mesh):
    return jax.shard_map(
        on_device,
        mesh=mesh,
        in_specs=(
            P(None, "slab", "tile", None),
            P("slab", None, "tile", None),
            P("tile", None),
            P(),
        ),
        out_specs=P("slab", None, None, "tile", None),
        check_vma=False,
    )
```

```python
import math

import jax
import jax.numpy as jnp
from jax import lax
from jax.sharding import PartitionSpec as P

SWEEPS = 2
H = 8


DIFFUSE = 0.15


def passed_along(block, axis, distance):
    devices = range(lax.axis_size(axis))
    route = [((i - distance) % len(devices), i) for i in devices]
    return lax.ppermute(block, axis, route)


def with_neighbours(block, axis, dim):
    count = lax.axis_size(axis)
    before = lax.ppermute(block, axis, [(i, i + 1) for i in range(count - 1)])
    after = lax.ppermute(block, axis, [(i + 1, i) for i in range(count - 1)])
    return jnp.concatenate([before, block, after], axis=dim)


def pad_grid(field):
    widths = [(0, 0)] * (field.ndim - 2) + [(1, 1), (1, 1)]
    return jnp.pad(field, widths)


def laplace(padded, center):
    return (
        padded[..., 2:, 1:-1]
        + padded[..., :-2, 1:-1]
        + padded[..., 1:-1, 2:]
        + padded[..., 1:-1, :-2]
        - 4.0 * center
    )


def forward_rate(state, speed_x, speed_y, damping, source, mask):
    padded = pad_grid(state)
    grad_x = 0.5 * (padded[..., 2:, 1:-1] - padded[..., :-2, 1:-1])
    grad_y = 0.5 * (padded[..., 1:-1, 2:] - padded[..., 1:-1, :-2])
    rate = source - (speed_x * grad_x + speed_y * grad_y) + DIFFUSE * laplace(padded, state) - damping * state
    return rate * mask


def adjoint_rate(state, speed_x, speed_y, damping, source, mask):
    padded = pad_grid(state)
    flux_x = pad_grid(speed_x * state)
    flux_y = pad_grid(speed_y * state)
    div_x = 0.5 * (flux_x[..., 2:, 1:-1] - flux_x[..., :-2, 1:-1])
    div_y = 0.5 * (flux_y[..., 1:-1, 2:] - flux_y[..., 1:-1, :-2])
    rate = source + div_x + div_y + DIFFUSE * laplace(padded, state) - damping * state
    return rate * mask


def coefficient_table(chosen, phase, periods):
    turns = chosen[:, None] * phase[None, :] % periods
    angle = 2.0 * math.pi / periods * turns.astype(jnp.float32)
    table = jnp.stack([jnp.cos(angle), -jnp.sin(angle)], axis=1) * (1.0 / math.sqrt(periods))
    return table.reshape(2 * chosen.shape[0], phase.shape[0])


def on_device(base_flow, forcing, damping, harmonics):
    steps = forcing.shape[0]
    count_f, rows, columns = (forcing.shape[1], forcing.shape[2], forcing.shape[3])
    slabs = lax.axis_size("slab")
    tiles = lax.axis_size("tile")
    periods = steps * slabs

    packed = jnp.concatenate(
        [base_flow.reshape(2 * steps, rows, columns), forcing.reshape(steps * count_f, rows, columns), damping[None]],
        axis=0,
    )
    wide = with_neighbours(packed, "tile", 1)
    ext = 3 * rows
    flow = wide[: 2 * steps].reshape(2, steps, ext, columns)
    drive = wide[2 * steps : 2 * steps + steps * count_f].reshape(steps, count_f, ext, columns)
    damp = wide[-1]
    row = lax.axis_index("tile") * rows - rows + jnp.arange(ext, dtype=jnp.int32)
    mask = ((row >= 0) & (row < tiles * rows)).astype(jnp.float32)[:, None]

    start = jnp.zeros((count_f, ext, columns), jnp.float32)
    for sweep in range(SWEEPS):
        state = start
        record = []
        for step in range(steps):
            record.append(state)
            speed_x = flow[0, step]
            speed_y = flow[1, step]
            first = forward_rate(state, speed_x, speed_y, damp, drive[step], mask)
            second = forward_rate(state + first, speed_x, speed_y, damp, drive[step], mask)
            state = state + 0.5 * (first + second)
        if sweep + 1 < SWEEPS:
            start = passed_along(state, "slab", 1)
    response = record
    start = jnp.zeros((count_f, ext, columns), jnp.float32)
    for sweep in range(SWEEPS):
        state = start
        record = [None] * steps
        for step in range(steps - 1, -1, -1):
            speed_x = flow[0, step]
            speed_y = flow[1, step]
            first = adjoint_rate(state, speed_x, speed_y, damp, response[step], mask)
            second = adjoint_rate(state + first, speed_x, speed_y, damp, response[step], mask)
            state = state + 0.5 * (first + second)
            record[step] = state
        if sweep + 1 < SWEEPS:
            keep = passed_along(state[:, rows // 2 : ext - rows // 2], "slab", -1)
            start = jnp.pad(keep, ((0, 0), (rows // 2, rows // 2), (0, 0)))
    adjoint = jnp.stack(record, axis=0)[:, :, rows : 2 * rows]
    phase = lax.axis_index("slab") * steps + jnp.arange(steps, dtype=jnp.int32)
    flat = adjoint.reshape(steps, count_f * rows * columns)
    table = coefficient_table(harmonics, phase, periods)
    terms = jnp.dot(table, flat, precision=lax.Precision.HIGHEST)
    parts = lax.all_to_all(terms.reshape(slabs, 2 * H // slabs, count_f, rows, columns), "slab", 0, 0, tiled=True)
    return jnp.sum(parts, axis=0, keepdims=True)


def solution(mesh):
    return jax.shard_map(
        on_device,
        mesh=mesh,
        in_specs=(
            P(None, "slab", "tile", None),
            P("slab", None, "tile", None),
            P("tile", None),
            P(),
        ),
        out_specs=P("slab", None, None, "tile", None),
        check_vma=False,
    )
```

```python
import math

import jax
import jax.numpy as jnp
from jax import lax
from jax.sharding import PartitionSpec as P

SWEEPS = 2
H = 8


DIFFUSE = 0.15


def passed_along(block, axis, distance):
    devices = range(lax.axis_size(axis))
    route = [((i - distance) % len(devices), i) for i in devices]
    return lax.ppermute(block, axis, route)


def with_neighbours(block, axis, dim):
    count = lax.axis_size(axis)
    before = lax.ppermute(block, axis, [(i, i + 1) for i in range(count - 1)])
    after = lax.ppermute(block, axis, [(i + 1, i) for i in range(count - 1)])
    return jnp.concatenate([before, block, after], axis=dim)


def pad_grid(field):
    widths = [(0, 0)] * (field.ndim - 2) + [(1, 1), (1, 1)]
    return jnp.pad(field, widths)


def laplace(padded, center):
    return (
        padded[..., 2:, 1:-1]
        + padded[..., :-2, 1:-1]
        + padded[..., 1:-1, 2:]
        + padded[..., 1:-1, :-2]
        - 4.0 * center
    )


def forward_rate(state, speed_x, speed_y, damping, source, mask):
    padded = pad_grid(state)
    grad_x = 0.5 * (padded[..., 2:, 1:-1] - padded[..., :-2, 1:-1])
    grad_y = 0.5 * (padded[..., 1:-1, 2:] - padded[..., 1:-1, :-2])
    rate = source - (speed_x * grad_x + speed_y * grad_y) + DIFFUSE * laplace(padded, state) - damping * state
    return rate * mask


def adjoint_rate(state, speed_x, speed_y, damping, source, mask):
    padded = pad_grid(state)
    flux_x = pad_grid(speed_x * state)
    flux_y = pad_grid(speed_y * state)
    div_x = 0.5 * (flux_x[..., 2:, 1:-1] - flux_x[..., :-2, 1:-1])
    div_y = 0.5 * (flux_y[..., 1:-1, 2:] - flux_y[..., 1:-1, :-2])
    rate = source + div_x + div_y + DIFFUSE * laplace(padded, state) - damping * state
    return rate * mask


def coefficient_table(chosen, phase, periods):
    turns = chosen[:, None] * phase[None, :] % periods
    angle = 2.0 * math.pi / periods * turns.astype(jnp.float32)
    table = jnp.stack([jnp.cos(angle), -jnp.sin(angle)], axis=1) * (1.0 / math.sqrt(periods))
    return table.reshape(2 * chosen.shape[0], phase.shape[0])


def on_device(base_flow, forcing, damping, harmonics):
    steps = forcing.shape[0]
    count_f, rows, columns = (forcing.shape[1], forcing.shape[2], forcing.shape[3])
    slabs = lax.axis_size("slab")
    tiles = lax.axis_size("tile")
    periods = steps * slabs

    packed = jnp.concatenate(
        [base_flow.reshape(2 * steps, rows, columns), forcing.reshape(steps * count_f, rows, columns), damping[None]],
        axis=0,
    )
    wide = with_neighbours(packed, "tile", 1)
    ext = 3 * rows
    flow = wide[: 2 * steps].reshape(2, steps, ext, columns)
    drive = wide[2 * steps : 2 * steps + steps * count_f].reshape(steps, count_f, ext, columns)
    damp = wide[-1]
    row = lax.axis_index("tile") * rows - rows + jnp.arange(ext, dtype=jnp.int32)
    mask = ((row >= 0) & (row < tiles * rows)).astype(jnp.float32)[:, None]

    def band(depth):
        return min(rows, -(-depth // 8) * 8)

    def cut(field, have, want):
        return lax.slice_in_dim(field, have - want, have + rows + want, axis=field.ndim - 2)

    def full(field, want):
        return cut(field, rows, want)

    tail = 2 * steps
    fwd_need = [tail + 4 * steps - 3 - 2 * m for m in range(steps)]
    fwd_need = [max(need, tail + 2 * m + 2) for m, need in enumerate(fwd_need)]
    sweep_bands = [
        [band(fwd_need[0] + 2 * (steps - m)) for m in range(steps)],
        [band(need) for need in fwd_need],
    ]
    sends = [band(fwd_need[0])]

    have = band(fwd_need[0] + 2 * steps)
    start = jnp.zeros((count_f, rows + 2 * have, columns), jnp.float32)
    for sweep in range(SWEEPS):
        state = start
        record = []
        for step in range(steps):
            want = sweep_bands[min(sweep, 1)][step]
            state = cut(state, have, want)
            have = want
            record.append((state, have))
            speed_x = full(flow[0, step], want)
            speed_y = full(flow[1, step], want)
            damp_here, mask_here = full(damp, want), full(mask, want)
            source = full(drive[step], want)
            first = forward_rate(state, speed_x, speed_y, damp_here, source, mask_here)
            second = forward_rate(state + first, speed_x, speed_y, damp_here, source, mask_here)
            state = state + 0.5 * (first + second)
        if sweep + 1 < SWEEPS:
            start = passed_along(cut(state, have, sends[0]), "slab", 1)
            have = sends[0]
    response = record
    adj_bands = [
        [band(tail + 2 * m + 2) for m in range(steps)],
        [band(2 * m + 2) for m in range(steps)],
    ]
    have = adj_bands[0][steps - 1]
    start = jnp.zeros((count_f, rows + 2 * have, columns), jnp.float32)
    for sweep in range(SWEEPS):
        state = start
        record = [None] * steps
        for step in range(steps - 1, -1, -1):
            want = adj_bands[min(sweep, 1)][step]
            state = cut(state, have, want)
            have = want
            speed_x = full(flow[0, step], want)
            speed_y = full(flow[1, step], want)
            damp_here, mask_here = full(damp, want), full(mask, want)
            source = cut(response[step][0], response[step][1], want)
            first = adjoint_rate(state, speed_x, speed_y, damp_here, source, mask_here)
            second = adjoint_rate(state + first, speed_x, speed_y, damp_here, source, mask_here)
            state = state + 0.5 * (first + second)
            record[step] = cut(state, have, 0)
        if sweep + 1 < SWEEPS:
            start = passed_along(cut(state, have, tail), "slab", -1)
            have = tail
    adjoint = jnp.stack(record, axis=0)
    phase = lax.axis_index("slab") * steps + jnp.arange(steps, dtype=jnp.int32)
    flat = adjoint.reshape(steps, count_f * rows * columns)
    table = coefficient_table(harmonics, phase, periods)
    terms = jnp.dot(table, flat, precision=lax.Precision.HIGHEST)
    parts = lax.all_to_all(terms.reshape(slabs, 2 * H // slabs, count_f, rows, columns), "slab", 0, 0, tiled=True)
    return jnp.sum(parts, axis=0, keepdims=True)


def solution(mesh):
    return jax.shard_map(
        on_device,
        mesh=mesh,
        in_specs=(
            P(None, "slab", "tile", None),
            P("slab", None, "tile", None),
            P("tile", None),
            P(),
        ),
        out_specs=P("slab", None, None, "tile", None),
        check_vma=False,
    )
```

```python
import math

import jax
import jax.numpy as jnp
from jax import lax
from jax.sharding import PartitionSpec as P

SWEEPS = 2
H = 8


DIFFUSE = 0.15


def passed_along(block, axis, distance):
    devices = range(lax.axis_size(axis))
    route = [((i - distance) % len(devices), i) for i in devices]
    return lax.ppermute(block, axis, route)


def with_neighbours(block, axis, dim):
    count = lax.axis_size(axis)
    before = lax.ppermute(block, axis, [(i, i + 1) for i in range(count - 1)])
    after = lax.ppermute(block, axis, [(i + 1, i) for i in range(count - 1)])
    return jnp.concatenate([before, block, after], axis=dim)


def pad_grid(field):
    widths = [(0, 0)] * (field.ndim - 2) + [(1, 1), (1, 1)]
    return jnp.pad(field, widths)


def laplace(padded, center):
    return (
        padded[..., 2:, 1:-1]
        + padded[..., :-2, 1:-1]
        + padded[..., 1:-1, 2:]
        + padded[..., 1:-1, :-2]
        - 4.0 * center
    )


def forward_rate(state, speed_x, speed_y, damping, source, mask):
    padded = pad_grid(state)
    grad_x = 0.5 * (padded[..., 2:, 1:-1] - padded[..., :-2, 1:-1])
    grad_y = 0.5 * (padded[..., 1:-1, 2:] - padded[..., 1:-1, :-2])
    rate = source - (speed_x * grad_x + speed_y * grad_y) + DIFFUSE * laplace(padded, state) - damping * state
    return rate * mask


def adjoint_rate(state, speed_x, speed_y, damping, source, mask):
    padded = pad_grid(state)
    flux_x = pad_grid(speed_x * state)
    flux_y = pad_grid(speed_y * state)
    div_x = 0.5 * (flux_x[..., 2:, 1:-1] - flux_x[..., :-2, 1:-1])
    div_y = 0.5 * (flux_y[..., 1:-1, 2:] - flux_y[..., 1:-1, :-2])
    rate = source + div_x + div_y + DIFFUSE * laplace(padded, state) - damping * state
    return rate * mask


def coefficient_table(chosen, phase, periods):
    turns = chosen[:, None] * phase[None, :] % periods
    angle = 2.0 * math.pi / periods * turns.astype(jnp.float32)
    table = jnp.stack([jnp.cos(angle), -jnp.sin(angle)], axis=1) * (1.0 / math.sqrt(periods))
    return table.reshape(2 * chosen.shape[0], phase.shape[0])


def on_device(base_flow, forcing, damping, harmonics):
    steps = forcing.shape[0]
    count_f, rows, columns = (forcing.shape[1], forcing.shape[2], forcing.shape[3])
    slabs = lax.axis_size("slab")
    tiles = lax.axis_size("tile")
    periods = steps * slabs

    packed = jnp.concatenate(
        [base_flow.reshape(2 * steps, rows, columns), forcing.reshape(steps * count_f, rows, columns), damping[None]],
        axis=0,
    )

    def band(depth):
        return min(rows, -(-depth // 8) * 8)

    def cut(field, have, want):
        return lax.slice_in_dim(field, have - want, have + rows + want, axis=field.ndim - 2)

    tail = 2 * steps
    fwd_need = [tail + 4 * steps - 3 - 2 * m for m in range(steps)]
    fwd_need = [max(need, tail + 2 * m + 2) for m, need in enumerate(fwd_need)]
    near = band(2 * steps)
    far = band(fwd_need[0])

    before = lax.ppermute(packed[:, rows - near :], "tile", [(i, i + 1) for i in range(tiles - 1)])
    after = lax.ppermute(packed[:, :near], "tile", [(i + 1, i) for i in range(tiles - 1)])
    before_far = lax.ppermute(packed[:, rows - far : rows - near], "tile", [(i, i + 1) for i in range(tiles - 1)])
    after_far = lax.ppermute(packed[:, near:far], "tile", [(i + 1, i) for i in range(tiles - 1)])
    narrow = jnp.concatenate([before, packed, after], axis=1)
    wide = jnp.concatenate([before_far, before, packed, after, after_far], axis=1)

    def fields(block, have):
        ext = rows + 2 * have
        flow = block[: 2 * steps].reshape(2, steps, ext, columns)
        drive = block[2 * steps : 2 * steps + steps * count_f].reshape(steps, count_f, ext, columns)
        row = lax.axis_index("tile") * rows - have + jnp.arange(ext, dtype=jnp.int32)
        mask = ((row >= 0) & (row < tiles * rows)).astype(jnp.float32)[:, None]
        return flow, drive, block[-1], mask, have

    sweep_fields = [fields(narrow, near), fields(wide, far)]
    sweep_bands = [
        [band(2 * (steps - m)) for m in range(steps)],
        [band(need) for need in fwd_need],
    ]

    have = sweep_bands[0][0]
    start = jnp.zeros((count_f, rows + 2 * have, columns), jnp.float32)
    for sweep in range(SWEEPS):
        flow, drive, damp, mask, held = sweep_fields[min(sweep, 1)]
        state = start
        record = []
        for step in range(steps):
            want = sweep_bands[min(sweep, 1)][step]
            state = cut(state, have, want)
            have = want
            record.append((state, have))
            speed_x = cut(flow[0, step], held, want)
            speed_y = cut(flow[1, step], held, want)
            damp_here, mask_here = cut(damp, held, want), cut(mask, held, want)
            source = cut(drive[step], held, want)
            first = forward_rate(state, speed_x, speed_y, damp_here, source, mask_here)
            second = forward_rate(state + first, speed_x, speed_y, damp_here, source, mask_here)
            state = state + 0.5 * (first + second)
        if sweep + 1 < SWEEPS:
            own = cut(state, have, 0)
            ahead = lambda j, t: ((j + 1) % slabs) * tiles + t
            up = lax.ppermute(own[:, rows - far :], ("slab", "tile"),
                              [(j * tiles + t, ahead(j, t + 1)) for j in range(slabs) for t in range(tiles - 1)])
            down = lax.ppermute(own[:, :far], ("slab", "tile"),
                                [(j * tiles + t + 1, ahead(j, t)) for j in range(slabs) for t in range(tiles - 1)])
            start = jnp.concatenate([up, passed_along(own, "slab", 1), down], axis=1)
            have = far
    response = record
    adj_bands = [
        [band(tail + 2 * m + 2) for m in range(steps)],
        [band(2 * m + 2) for m in range(steps)],
    ]
    flow, drive, damp, mask, held = sweep_fields[1]
    have = adj_bands[0][steps - 1]
    start = jnp.zeros((count_f, rows + 2 * have, columns), jnp.float32)
    for sweep in range(SWEEPS):
        state = start
        record = [None] * steps
        for step in range(steps - 1, -1, -1):
            want = adj_bands[min(sweep, 1)][step]
            state = cut(state, have, want)
            have = want
            speed_x = cut(flow[0, step], held, want)
            speed_y = cut(flow[1, step], held, want)
            damp_here, mask_here = cut(damp, held, want), cut(mask, held, want)
            source = cut(response[step][0], response[step][1], want)
            first = adjoint_rate(state, speed_x, speed_y, damp_here, source, mask_here)
            second = adjoint_rate(state + first, speed_x, speed_y, damp_here, source, mask_here)
            state = state + 0.5 * (first + second)
            record[step] = cut(state, have, 0)
        if sweep + 1 < SWEEPS:
            start = passed_along(cut(state, have, tail), "slab", -1)
            have = tail
    adjoint = jnp.stack(record, axis=0)
    phase = lax.axis_index("slab") * steps + jnp.arange(steps, dtype=jnp.int32)
    flat = adjoint.reshape(steps, count_f * rows * columns)
    table = coefficient_table(harmonics, phase, periods)
    terms = jnp.dot(table, flat, precision=lax.Precision.HIGHEST)
    parts = lax.all_to_all(terms.reshape(slabs, 2 * H // slabs, count_f, rows, columns), "slab", 0, 0, tiled=True)
    return jnp.sum(parts, axis=0, keepdims=True)


def solution(mesh):
    return jax.shard_map(
        on_device,
        mesh=mesh,
        in_specs=(
            P(None, "slab", "tile", None),
            P("slab", None, "tile", None),
            P("tile", None),
            P(),
        ),
        out_specs=P("slab", None, None, "tile", None),
        check_vma=False,
    )
```

```python
import math

import jax
import jax.numpy as jnp
from jax import lax
from jax.sharding import PartitionSpec as P

SWEEPS = 2
H = 8


DIFFUSE = 0.15


def passed_along(block, axis, distance):
    devices = range(lax.axis_size(axis))
    route = [((i - distance) % len(devices), i) for i in devices]
    return lax.ppermute(block, axis, route)


def with_neighbours(block, axis, dim):
    count = lax.axis_size(axis)
    before = lax.ppermute(block, axis, [(i, i + 1) for i in range(count - 1)])
    after = lax.ppermute(block, axis, [(i + 1, i) for i in range(count - 1)])
    return jnp.concatenate([before, block, after], axis=dim)


def pad_grid(field):
    widths = [(0, 0)] * (field.ndim - 2) + [(1, 1), (1, 1)]
    return jnp.pad(field, widths)


def laplace(padded, center):
    return (
        padded[..., 2:, 1:-1]
        + padded[..., :-2, 1:-1]
        + padded[..., 1:-1, 2:]
        + padded[..., 1:-1, :-2]
        - 4.0 * center
    )


def forward_rate(state, speed_x, speed_y, damping, source, mask):
    padded = pad_grid(state)
    grad_x = 0.5 * (padded[..., 2:, 1:-1] - padded[..., :-2, 1:-1])
    grad_y = 0.5 * (padded[..., 1:-1, 2:] - padded[..., 1:-1, :-2])
    rate = source - (speed_x * grad_x + speed_y * grad_y) + DIFFUSE * laplace(padded, state) - damping * state
    return rate * mask


def adjoint_rate(state, speed_x, speed_y, damping, source, mask):
    padded = pad_grid(state)
    flux_x = pad_grid(speed_x * state)
    flux_y = pad_grid(speed_y * state)
    div_x = 0.5 * (flux_x[..., 2:, 1:-1] - flux_x[..., :-2, 1:-1])
    div_y = 0.5 * (flux_y[..., 1:-1, 2:] - flux_y[..., 1:-1, :-2])
    rate = source + div_x + div_y + DIFFUSE * laplace(padded, state) - damping * state
    return rate * mask


def coefficient_table(chosen, phase, periods):
    turns = chosen[:, None] * phase[None, :] % periods
    angle = 2.0 * math.pi / periods * turns.astype(jnp.float32)
    table = jnp.stack([jnp.cos(angle), -jnp.sin(angle)], axis=1) * (1.0 / math.sqrt(periods))
    return table.reshape(2 * chosen.shape[0], phase.shape[0])


def on_device(base_flow, forcing, damping, harmonics):
    steps = forcing.shape[0]
    count_f, rows, columns = (forcing.shape[1], forcing.shape[2], forcing.shape[3])
    slabs = lax.axis_size("slab")
    tiles = lax.axis_size("tile")
    periods = steps * slabs

    packed = jnp.concatenate(
        [base_flow.reshape(2 * steps, rows, columns), forcing.reshape(steps * count_f, rows, columns), damping[None]],
        axis=0,
    )

    def band(depth):
        return min(rows, -(-depth // 8) * 8)

    def cut(field, have, want):
        return lax.slice_in_dim(field, have - want, have + rows + want, axis=field.ndim - 2)

    tail = 2 * steps
    fwd_need = [tail + 4 * steps - 3 - 2 * m for m in range(steps)]
    fwd_need = [max(need, tail + 2 * m + 2) for m, need in enumerate(fwd_need)]
    near = band(2 * steps)
    far = band(fwd_need[0])

    before = lax.ppermute(packed[:, rows - far :], "tile", [(i, i + 1) for i in range(tiles - 1)])
    after = lax.ppermute(packed[:, :far], "tile", [(i + 1, i) for i in range(tiles - 1)])
    wide = jnp.concatenate([before, packed, after], axis=1)

    def fields(block, have):
        ext = rows + 2 * have
        flow = block[: 2 * steps].reshape(2, steps, ext, columns)
        drive = block[2 * steps : 2 * steps + steps * count_f].reshape(steps, count_f, ext, columns)
        row = lax.axis_index("tile") * rows - have + jnp.arange(ext, dtype=jnp.int32)
        mask = ((row >= 0) & (row < tiles * rows)).astype(jnp.float32)[:, None]
        return flow, drive, block[-1], mask, have

    sweep_fields = [fields(wide, far)] * 2
    sweep_bands = [
        [band(2 * (steps - m)) for m in range(steps)],
        [band(need) for need in fwd_need],
    ]

    have = sweep_bands[0][0]
    start = jnp.zeros((count_f, rows + 2 * have, columns), jnp.float32)
    for sweep in range(SWEEPS):
        flow, drive, damp, mask, held = sweep_fields[min(sweep, 1)]
        state = start
        record = []
        for step in range(steps):
            want = sweep_bands[min(sweep, 1)][step]
            state = cut(state, have, want)
            have = want
            record.append((state, have))
            speed_x = cut(flow[0, step], held, want)
            speed_y = cut(flow[1, step], held, want)
            damp_here, mask_here = cut(damp, held, want), cut(mask, held, want)
            source = cut(drive[step], held, want)
            first = forward_rate(state, speed_x, speed_y, damp_here, source, mask_here)
            second = forward_rate(state + first, speed_x, speed_y, damp_here, source, mask_here)
            state = state + 0.5 * (first + second)
        if sweep + 1 < SWEEPS:
            own = cut(state, have, 0)
            ahead = lambda j, t: ((j + 1) % slabs) * tiles + t
            up = lax.ppermute(own[:, rows - far :], ("slab", "tile"),
                              [(j * tiles + t, ahead(j, t + 1)) for j in range(slabs) for t in range(tiles - 1)])
            down = lax.ppermute(own[:, :far], ("slab", "tile"),
                                [(j * tiles + t + 1, ahead(j, t)) for j in range(slabs) for t in range(tiles - 1)])
            start = jnp.concatenate([up, passed_along(own, "slab", 1), down], axis=1)
            have = far
    response = record
    adj_bands = [
        [band(tail + 2 * m + 2) for m in range(steps)],
        [band(2 * m + 2) for m in range(steps)],
    ]
    flow, drive, damp, mask, held = sweep_fields[1]
    have = adj_bands[0][steps - 1]
    start = jnp.zeros((count_f, rows + 2 * have, columns), jnp.float32)
    for sweep in range(SWEEPS):
        state = start
        record = [None] * steps
        for step in range(steps - 1, -1, -1):
            want = adj_bands[min(sweep, 1)][step]
            state = cut(state, have, want)
            have = want
            speed_x = cut(flow[0, step], held, want)
            speed_y = cut(flow[1, step], held, want)
            damp_here, mask_here = cut(damp, held, want), cut(mask, held, want)
            source = cut(response[step][0], response[step][1], want)
            first = adjoint_rate(state, speed_x, speed_y, damp_here, source, mask_here)
            second = adjoint_rate(state + first, speed_x, speed_y, damp_here, source, mask_here)
            state = state + 0.5 * (first + second)
            record[step] = cut(state, have, 0)
        if sweep + 1 < SWEEPS:
            start = passed_along(cut(state, have, tail), "slab", -1)
            have = tail
    adjoint = jnp.stack(record, axis=0)
    phase = lax.axis_index("slab") * steps + jnp.arange(steps, dtype=jnp.int32)
    flat = adjoint.reshape(steps, count_f * rows * columns)
    table = coefficient_table(harmonics, phase, periods)
    terms = jnp.dot(table, flat, precision=lax.Precision.HIGHEST)
    ring = 4
    rings = slabs // ring
    here = lax.axis_index("slab")
    split = terms.reshape(rings, ring, 2 * H // slabs, count_f, rows, columns).swapaxes(0, 1)
    groups = [list(range(g * ring, (g + 1) * ring)) for g in range(rings)]
    parts = lax.all_to_all(split, "slab", 0, 0, tiled=True, axis_index_groups=groups)
    partial = jnp.sum(parts, axis=0)
    total = lax.dynamic_index_in_dim(partial, here // ring, 0, keepdims=False)
    for shift in range(1, rings):
        away = lax.dynamic_index_in_dim(partial, (here // ring + shift) % rings, 0, keepdims=False)
        total = total + passed_along(away, "slab", shift * ring)
    return total[None]


def solution(mesh):
    return jax.shard_map(
        on_device,
        mesh=mesh,
        in_specs=(
            P(None, "slab", "tile", None),
            P("slab", None, "tile", None),
            P("tile", None),
            P(),
        ),
        out_specs=P("slab", None, None, "tile", None),
        check_vma=False,
    )
```

```python
import math

import jax
import jax.numpy as jnp
from jax import lax
from jax.sharding import PartitionSpec as P

SWEEPS = 2
H = 8


DIFFUSE = 0.15


def passed_along(block, axis, distance):
    devices = range(lax.axis_size(axis))
    route = [((i - distance) % len(devices), i) for i in devices]
    return lax.ppermute(block, axis, route)


def with_neighbours(block, axis, dim):
    count = lax.axis_size(axis)
    before = lax.ppermute(block, axis, [(i, i + 1) for i in range(count - 1)])
    after = lax.ppermute(block, axis, [(i + 1, i) for i in range(count - 1)])
    return jnp.concatenate([before, block, after], axis=dim)


def pad_grid(field):
    widths = [(0, 0)] * (field.ndim - 2) + [(1, 1), (1, 1)]
    return jnp.pad(field, widths)


def laplace(padded, center):
    return (
        padded[..., 2:, 1:-1]
        + padded[..., :-2, 1:-1]
        + padded[..., 1:-1, 2:]
        + padded[..., 1:-1, :-2]
        - 4.0 * center
    )


def forward_rate(state, speed_x, speed_y, damping, source, mask):
    padded = pad_grid(state)
    grad_x = 0.5 * (padded[..., 2:, 1:-1] - padded[..., :-2, 1:-1])
    grad_y = 0.5 * (padded[..., 1:-1, 2:] - padded[..., 1:-1, :-2])
    rate = source - (speed_x * grad_x + speed_y * grad_y) + DIFFUSE * laplace(padded, state) - damping * state
    return rate * mask


def adjoint_rate(state, speed_x, speed_y, damping, source, mask):
    padded = pad_grid(state)
    flux_x = pad_grid(speed_x * state)
    flux_y = pad_grid(speed_y * state)
    div_x = 0.5 * (flux_x[..., 2:, 1:-1] - flux_x[..., :-2, 1:-1])
    div_y = 0.5 * (flux_y[..., 1:-1, 2:] - flux_y[..., 1:-1, :-2])
    rate = source + div_x + div_y + DIFFUSE * laplace(padded, state) - damping * state
    return rate * mask


def coefficient_table(chosen, phase, periods):
    turns = chosen[:, None] * phase[None, :] % periods
    angle = 2.0 * math.pi / periods * turns.astype(jnp.float32)
    table = jnp.stack([jnp.cos(angle), -jnp.sin(angle)], axis=1) * (1.0 / math.sqrt(periods))
    return table.reshape(2 * chosen.shape[0], phase.shape[0])


def on_device(base_flow, forcing, damping, harmonics):
    steps = forcing.shape[0]
    count_f, rows, columns = (forcing.shape[1], forcing.shape[2], forcing.shape[3])
    slabs = lax.axis_size("slab")
    tiles = lax.axis_size("tile")
    periods = steps * slabs

    packed = jnp.concatenate(
        [base_flow.reshape(2 * steps, rows, columns), forcing.reshape(steps * count_f, rows, columns), damping[None]],
        axis=0,
    )

    def band(depth):
        return min(rows, -(-depth // 8) * 8)

    def cut(field, have, want):
        return lax.slice_in_dim(field, have - want, have + rows + want, axis=field.ndim - 2)

    tail = 2 * steps
    fwd_need = [tail + 4 * steps - 3 - 2 * m for m in range(steps)]
    fwd_need = [max(need, tail + 2 * m + 2) for m, need in enumerate(fwd_need)]
    far = band(fwd_need[0])

    before = lax.ppermute(packed[:, rows - far :], "tile", [(i, i + 1) for i in range(tiles - 1)])
    after = lax.ppermute(packed[:, :far], "tile", [(i + 1, i) for i in range(tiles - 1)])
    wide = jnp.concatenate([before, packed, after], axis=1)

    def fields(block, have):
        ext = rows + 2 * have
        flow = block[: 2 * steps].reshape(2, steps, ext, columns)
        drive = block[2 * steps : 2 * steps + steps * count_f].reshape(steps, count_f, ext, columns)
        row = lax.axis_index("tile") * rows - have + jnp.arange(ext, dtype=jnp.int32)
        mask = ((row >= 0) & (row < tiles * rows)).astype(jnp.float32)[:, None]
        return flow, drive, block[-1], mask, have

    sweep_fields = [fields(wide, far)] * 2
    sweep_bands = [
        [band(2 * (steps - m)) for m in range(steps)],
        [band(need) for need in fwd_need],
    ]

    have = sweep_bands[0][0]
    start = jnp.zeros((count_f, rows + 2 * have, columns), jnp.float32)
    for sweep in range(SWEEPS):
        flow, drive, damp, mask, held = sweep_fields[min(sweep, 1)]
        state = start
        record = []
        for step in range(steps):
            want = sweep_bands[min(sweep, 1)][step]
            state = cut(state, have, want)
            have = want
            record.append((state, have))
            speed_x = cut(flow[0, step], held, want)
            speed_y = cut(flow[1, step], held, want)
            damp_here, mask_here = cut(damp, held, want), cut(mask, held, want)
            source = cut(drive[step], held, want)
            first = forward_rate(state, speed_x, speed_y, damp_here, source, mask_here)
            second = forward_rate(state + first, speed_x, speed_y, damp_here, source, mask_here)
            state = state + 0.5 * (first + second)
        if sweep + 1 < SWEEPS:
            own = cut(state, have, 0)
            ahead = lambda j, t: ((j + 1) % slabs) * tiles + t
            up = lax.ppermute(own[:, rows - far :], ("slab", "tile"),
                              [(j * tiles + t, ahead(j, t + 1)) for j in range(slabs) for t in range(tiles - 1)])
            down = lax.ppermute(own[:, :far], ("slab", "tile"),
                                [(j * tiles + t + 1, ahead(j, t)) for j in range(slabs) for t in range(tiles - 1)])
            start = jnp.concatenate([up, passed_along(own, "slab", 1), down], axis=1)
            have = far
    response = record
    adj_bands = [
        [band(tail + 2 * m + 2) for m in range(steps)],
        [band(2 * m + 2) for m in range(steps)],
    ]
    flow, drive, damp, mask, held = sweep_fields[1]
    have = adj_bands[0][steps - 1]
    start = jnp.zeros((count_f, rows + 2 * have, columns), jnp.float32)
    for sweep in range(SWEEPS):
        state = start
        record = [None] * steps
        for step in range(steps - 1, -1, -1):
            want = adj_bands[min(sweep, 1)][step]
            state = cut(state, have, want)
            have = want
            speed_x = cut(flow[0, step], held, want)
            speed_y = cut(flow[1, step], held, want)
            damp_here, mask_here = cut(damp, held, want), cut(mask, held, want)
            source = cut(response[step][0], response[step][1], want)
            first = adjoint_rate(state, speed_x, speed_y, damp_here, source, mask_here)
            second = adjoint_rate(state + first, speed_x, speed_y, damp_here, source, mask_here)
            state = state + 0.5 * (first + second)
            record[step] = cut(state, have, 0)
        if sweep + 1 < SWEEPS:
            start = passed_along(cut(state, have, tail), "slab", -1)
            have = tail
    adjoint = jnp.stack(record, axis=0)
    phase = lax.axis_index("slab") * steps + jnp.arange(steps, dtype=jnp.int32)
    flat = adjoint.reshape(steps, count_f * rows * columns)
    table = coefficient_table(harmonics, phase, periods)
    terms = jnp.dot(table, flat, precision=lax.Precision.HIGHEST)
    parts = lax.all_to_all(terms.reshape(slabs, 2 * H // slabs, count_f, rows, columns), "slab", 0, 0, tiled=True)
    return jnp.sum(parts, axis=0, keepdims=True)


def solution(mesh):
    return jax.shard_map(
        on_device,
        mesh=mesh,
        in_specs=(
            P(None, "slab", "tile", None),
            P("slab", None, "tile", None),
            P("tile", None),
            P(),
        ),
        out_specs=P("slab", None, None, "tile", None),
        check_vma=False,
    )
```

```python
import math

import jax
import jax.numpy as jnp
from jax import lax
from jax.sharding import PartitionSpec as P

SWEEPS = 2
H = 8


DIFFUSE = 0.15


def passed_along(block, axis, distance):
    devices = range(lax.axis_size(axis))
    route = [((i - distance) % len(devices), i) for i in devices]
    return lax.ppermute(block, axis, route)


def with_neighbours(block, axis, dim):
    count = lax.axis_size(axis)
    before = lax.ppermute(block, axis, [(i, i + 1) for i in range(count - 1)])
    after = lax.ppermute(block, axis, [(i + 1, i) for i in range(count - 1)])
    return jnp.concatenate([before, block, after], axis=dim)


def pad_grid(field):
    widths = [(0, 0)] * (field.ndim - 2) + [(1, 1), (1, 1)]
    return jnp.pad(field, widths)


def laplace(padded, center):
    return (
        padded[..., 2:, 1:-1]
        + padded[..., :-2, 1:-1]
        + padded[..., 1:-1, 2:]
        + padded[..., 1:-1, :-2]
        - 4.0 * center
    )


def forward_rate(state, speed_x, speed_y, damping, source, mask):
    padded = pad_grid(state)
    grad_x = 0.5 * (padded[..., 2:, 1:-1] - padded[..., :-2, 1:-1])
    grad_y = 0.5 * (padded[..., 1:-1, 2:] - padded[..., 1:-1, :-2])
    rate = source - (speed_x * grad_x + speed_y * grad_y) + DIFFUSE * laplace(padded, state) - damping * state
    return rate * mask


def adjoint_rate(state, speed_x, speed_y, damping, source, mask):
    padded = pad_grid(state)
    flux_x = pad_grid(speed_x * state)
    flux_y = pad_grid(speed_y * state)
    div_x = 0.5 * (flux_x[..., 2:, 1:-1] - flux_x[..., :-2, 1:-1])
    div_y = 0.5 * (flux_y[..., 1:-1, 2:] - flux_y[..., 1:-1, :-2])
    rate = source + div_x + div_y + DIFFUSE * laplace(padded, state) - damping * state
    return rate * mask


def coefficient_table(chosen, phase, periods):
    turns = chosen[:, None] * phase[None, :] % periods
    angle = 2.0 * math.pi / periods * turns.astype(jnp.float32)
    table = jnp.stack([jnp.cos(angle), -jnp.sin(angle)], axis=1) * (1.0 / math.sqrt(periods))
    return table.reshape(2 * chosen.shape[0], phase.shape[0])


def on_device(base_flow, forcing, damping, harmonics):
    steps = forcing.shape[0]
    count_f, rows, columns = (forcing.shape[1], forcing.shape[2], forcing.shape[3])
    slabs = lax.axis_size("slab")
    tiles = lax.axis_size("tile")
    periods = steps * slabs

    def band(depth):
        return min(rows, -(-depth // 8) * 8)

    def cut(field, have, want):
        return lax.slice_in_dim(field, have - want, have + rows + want, axis=field.ndim - 2)

    def full(field, want):
        return cut(field, rows, want)

    tail = 2 * steps
    fwd_need = [tail + 4 * steps - 3 - 2 * m for m in range(steps)]
    fwd_need = [max(need, tail + 2 * m + 2) for m, need in enumerate(fwd_need)]
    step_depth = [band(fwd_need[0] + 2 * (steps - m) - 1) for m in range(steps)]
    assert max(step_depth) <= rows
    per_step = jnp.concatenate([base_flow.swapaxes(0, 1), forcing], axis=1)
    runs = []
    for m, d in enumerate(step_depth):
        if runs and runs[-1][2] == d:
            runs[-1][1] = m + 1
        else:
            runs.append([m, m + 1, d])

    def edges(take):
        pieces = [take(per_step[lo:hi], d).reshape(-1, columns) for lo, hi, d in runs]
        return jnp.concatenate(pieces + [take(damping, step_depth[0])], axis=0)

    down = lax.ppermute(edges(lambda x, d: x[..., rows - d :, :]), "tile", [(i, i + 1) for i in range(tiles - 1)])
    up = lax.ppermute(edges(lambda x, d: x[..., :d, :]), "tile", [(i + 1, i) for i in range(tiles - 1)])

    def placed(got, top):
        blocks, at = [], 0
        for lo, hi, d in runs:
            size = (hi - lo) * per_step.shape[1] * d
            block = got[at : at + size].reshape(hi - lo, per_step.shape[1], d, columns)
            gap = ((0, 0), (0, 0), (rows - d, 0) if top else (0, rows - d), (0, 0))
            blocks.append(jnp.pad(block, gap))
            at += size
        d = step_depth[0]
        damp_part = jnp.pad(got[at : at + d], ((rows - d, 0) if top else (0, rows - d), (0, 0)))
        return jnp.concatenate(blocks, axis=0), damp_part

    before, damp_before = placed(down, True)
    after, damp_after = placed(up, False)
    wide = jnp.concatenate([before, per_step, after], axis=2)
    ext = 3 * rows
    flow = wide[:, :2].swapaxes(0, 1)
    drive = wide[:, 2:]
    damp = jnp.concatenate([damp_before, damping, damp_after], axis=0)
    row = lax.axis_index("tile") * rows - rows + jnp.arange(ext, dtype=jnp.int32)
    mask = ((row >= 0) & (row < tiles * rows)).astype(jnp.float32)[:, None]

    sweep_bands = [
        [band(fwd_need[0] + 2 * (steps - m)) for m in range(steps)],
        [band(need) for need in fwd_need],
    ]
    sends = [band(fwd_need[0])]

    have = band(fwd_need[0] + 2 * steps)
    start = jnp.zeros((count_f, rows + 2 * have, columns), jnp.float32)
    for sweep in range(SWEEPS):
        state = start
        record = []
        for step in range(steps):
            want = sweep_bands[min(sweep, 1)][step]
            state = cut(state, have, want)
            have = want
            record.append((state, have))
            speed_x = full(flow[0, step], want)
            speed_y = full(flow[1, step], want)
            damp_here, mask_here = full(damp, want), full(mask, want)
            source = full(drive[step], want)
            first = forward_rate(state, speed_x, speed_y, damp_here, source, mask_here)
            second = forward_rate(state + first, speed_x, speed_y, damp_here, source, mask_here)
            state = state + 0.5 * (first + second)
        if sweep + 1 < SWEEPS:
            start = passed_along(cut(state, have, sends[0]), "slab", 1)
            have = sends[0]
    response = record
    adj_bands = [
        [band(tail + 2 * m + 2) for m in range(steps)],
        [band(2 * m + 2) for m in range(steps)],
    ]
    have = adj_bands[0][steps - 1]
    start = jnp.zeros((count_f, rows + 2 * have, columns), jnp.float32)
    for sweep in range(SWEEPS):
        state = start
        record = [None] * steps
        for step in range(steps - 1, -1, -1):
            want = adj_bands[min(sweep, 1)][step]
            state = cut(state, have, want)
            have = want
            speed_x = full(flow[0, step], want)
            speed_y = full(flow[1, step], want)
            damp_here, mask_here = full(damp, want), full(mask, want)
            source = cut(response[step][0], response[step][1], want)
            first = adjoint_rate(state, speed_x, speed_y, damp_here, source, mask_here)
            second = adjoint_rate(state + first, speed_x, speed_y, damp_here, source, mask_here)
            state = state + 0.5 * (first + second)
            record[step] = cut(state, have, 0)
        if sweep + 1 < SWEEPS:
            start = passed_along(cut(state, have, tail), "slab", -1)
            have = tail
    adjoint = jnp.stack(record, axis=0)
    phase = lax.axis_index("slab") * steps + jnp.arange(steps, dtype=jnp.int32)
    flat = adjoint.reshape(steps, count_f * rows * columns)
    table = coefficient_table(harmonics, phase, periods)
    terms = jnp.dot(table, flat, precision=lax.Precision.HIGHEST)
    parts = lax.all_to_all(terms.reshape(slabs, 2 * H // slabs, count_f, rows, columns), "slab", 0, 0, tiled=True)
    return jnp.sum(parts, axis=0, keepdims=True)


def solution(mesh):
    return jax.shard_map(
        on_device,
        mesh=mesh,
        in_specs=(
            P(None, "slab", "tile", None),
            P("slab", None, "tile", None),
            P("tile", None),
            P(),
        ),
        out_specs=P("slab", None, None, "tile", None),
        check_vma=False,
    )
```

```python
import math

import jax
import jax.numpy as jnp
from jax import lax
from jax.sharding import PartitionSpec as P

SWEEPS = 2
H = 8


DIFFUSE = 0.15


def passed_along(block, axis, distance):
    devices = range(lax.axis_size(axis))
    route = [((i - distance) % len(devices), i) for i in devices]
    return lax.ppermute(block, axis, route)


def with_neighbours(block, axis, dim):
    count = lax.axis_size(axis)
    before = lax.ppermute(block, axis, [(i, i + 1) for i in range(count - 1)])
    after = lax.ppermute(block, axis, [(i + 1, i) for i in range(count - 1)])
    return jnp.concatenate([before, block, after], axis=dim)


def pad_grid(field):
    widths = [(0, 0)] * (field.ndim - 2) + [(1, 1), (1, 1)]
    return jnp.pad(field, widths)


def laplace(padded, center):
    return (
        padded[..., 2:, 1:-1]
        + padded[..., :-2, 1:-1]
        + padded[..., 1:-1, 2:]
        + padded[..., 1:-1, :-2]
        - 4.0 * center
    )


def forward_rate(state, speed_x, speed_y, damping, source, mask):
    padded = pad_grid(state)
    grad_x = 0.5 * (padded[..., 2:, 1:-1] - padded[..., :-2, 1:-1])
    grad_y = 0.5 * (padded[..., 1:-1, 2:] - padded[..., 1:-1, :-2])
    rate = source - (speed_x * grad_x + speed_y * grad_y) + DIFFUSE * laplace(padded, state) - damping * state
    return rate * mask


def adjoint_rate(state, speed_x, speed_y, damping, source, mask):
    padded = pad_grid(state)
    flux_x = pad_grid(speed_x * state)
    flux_y = pad_grid(speed_y * state)
    div_x = 0.5 * (flux_x[..., 2:, 1:-1] - flux_x[..., :-2, 1:-1])
    div_y = 0.5 * (flux_y[..., 1:-1, 2:] - flux_y[..., 1:-1, :-2])
    rate = source + div_x + div_y + DIFFUSE * laplace(padded, state) - damping * state
    return rate * mask


def coefficient_table(chosen, phase, periods):
    turns = chosen[:, None] * phase[None, :] % periods
    angle = 2.0 * math.pi / periods * turns.astype(jnp.float32)
    table = jnp.stack([jnp.cos(angle), -jnp.sin(angle)], axis=1) * (1.0 / math.sqrt(periods))
    return table.reshape(2 * chosen.shape[0], phase.shape[0])


def on_device(base_flow, forcing, damping, harmonics):
    steps = forcing.shape[0]
    count_f, rows, columns = (forcing.shape[1], forcing.shape[2], forcing.shape[3])
    slabs = lax.axis_size("slab")
    tiles = lax.axis_size("tile")
    periods = steps * slabs

    packed = jnp.concatenate(
        [base_flow.reshape(2 * steps, rows, columns), forcing.reshape(steps * count_f, rows, columns), damping[None]],
        axis=0,
    )

    def band(depth):
        return min(rows, -(-depth // 8) * 8)

    def cut(field, have, want):
        return lax.slice_in_dim(field, have - want, have + rows + want, axis=field.ndim - 2)

    tail = 2 * steps
    fwd_need = [0] * steps
    fwd_need[-1] = 2 * steps - 1
    for m in range(steps - 2, -1, -1):
        fwd_need[m] = max(2 * m + 1, fwd_need[m + 1] + 2)
    fwd_need = [max(need, 2 * m + 2) for m, need in enumerate(fwd_need)]
    far = band(fwd_need[0])
    assert far <= rows

    before = lax.ppermute(packed[:, rows - far :], "tile", [(i, i + 1) for i in range(tiles - 1)])
    after = lax.ppermute(packed[:, :far], "tile", [(i + 1, i) for i in range(tiles - 1)])
    wide = jnp.concatenate([before, packed, after], axis=1)

    def fields(block, have):
        ext = rows + 2 * have
        flow = block[: 2 * steps].reshape(2, steps, ext, columns)
        drive = block[2 * steps : 2 * steps + steps * count_f].reshape(steps, count_f, ext, columns)
        row = lax.axis_index("tile") * rows - have + jnp.arange(ext, dtype=jnp.int32)
        mask = ((row >= 0) & (row < tiles * rows)).astype(jnp.float32)[:, None]
        return flow, drive, block[-1], mask, have

    sweep_fields = [fields(wide, far)] * 2
    def slab_start(own, shift, depth):
        onward = lambda j, t: ((j + shift) % slabs) * tiles + t
        both = ("slab", "tile")
        up = lax.ppermute(own[:, rows - depth :], both,
                          [(j * tiles + t, onward(j, t + 1)) for j in range(slabs) for t in range(tiles - 1)])
        down = lax.ppermute(own[:, :depth], both,
                            [(j * tiles + t + 1, onward(j, t)) for j in range(slabs) for t in range(tiles - 1)])
        return jnp.concatenate([up, passed_along(own, "slab", shift), down], axis=1)

    sweep_bands = [
        [band(2 * (steps - m)) for m in range(steps)],
        [band(need) for need in fwd_need],
    ]

    have = sweep_bands[0][0]
    start = jnp.zeros((count_f, rows + 2 * have, columns), jnp.float32)
    for sweep in range(SWEEPS):
        flow, drive, damp, mask, held = sweep_fields[min(sweep, 1)]
        state = start
        record = []
        for step in range(steps):
            want = sweep_bands[min(sweep, 1)][step]
            state = cut(state, have, want)
            have = want
            record.append((state, have))
            speed_x = cut(flow[0, step], held, want)
            speed_y = cut(flow[1, step], held, want)
            damp_here, mask_here = cut(damp, held, want), cut(mask, held, want)
            source = cut(drive[step], held, want)
            first = forward_rate(state, speed_x, speed_y, damp_here, source, mask_here)
            second = forward_rate(state + first, speed_x, speed_y, damp_here, source, mask_here)
            state = state + 0.5 * (first + second)
        if sweep + 1 < SWEEPS:
            start = slab_start(cut(state, have, 0), 1, far)
            have = far
    response = record
    adj_bands = [
        [band(2 * m + 2) for m in range(steps)],
        [band(2 * m + 2) for m in range(steps)],
    ]
    flow, drive, damp, mask, held = sweep_fields[1]
    have = adj_bands[0][steps - 1]
    start = jnp.zeros((count_f, rows + 2 * have, columns), jnp.float32)
    for sweep in range(SWEEPS):
        state = start
        record = [None] * steps
        for step in range(steps - 1, -1, -1):
            want = adj_bands[min(sweep, 1)][step]
            state = cut(state, have, want)
            have = want
            speed_x = cut(flow[0, step], held, want)
            speed_y = cut(flow[1, step], held, want)
            damp_here, mask_here = cut(damp, held, want), cut(mask, held, want)
            source = cut(response[step][0], response[step][1], want)
            first = adjoint_rate(state, speed_x, speed_y, damp_here, source, mask_here)
            second = adjoint_rate(state + first, speed_x, speed_y, damp_here, source, mask_here)
            state = state + 0.5 * (first + second)
            record[step] = cut(state, have, 0)
        if sweep + 1 < SWEEPS:
            start = slab_start(cut(state, have, 0), -1, tail)
            have = tail
    adjoint = jnp.stack(record, axis=0)
    phase = lax.axis_index("slab") * steps + jnp.arange(steps, dtype=jnp.int32)
    flat = adjoint.reshape(steps, count_f * rows * columns)
    table = coefficient_table(harmonics, phase, periods)
    terms = jnp.dot(table, flat, precision=lax.Precision.HIGHEST)
    parts = lax.all_to_all(terms.reshape(slabs, 2 * H // slabs, count_f, rows, columns), "slab", 0, 0, tiled=True)
    return jnp.sum(parts, axis=0, keepdims=True)


def solution(mesh):
    return jax.shard_map(
        on_device,
        mesh=mesh,
        in_specs=(
            P(None, "slab", "tile", None),
            P("slab", None, "tile", None),
            P("tile", None),
            P(),
        ),
        out_specs=P("slab", None, None, "tile", None),
        check_vma=False,
    )
```

```python
import math

import jax
import jax.numpy as jnp
from jax import lax
from jax.sharding import PartitionSpec as P

SWEEPS = 2
H = 8


DIFFUSE = 0.15


def passed_along(block, axis, distance):
    devices = range(lax.axis_size(axis))
    route = [((i - distance) % len(devices), i) for i in devices]
    return lax.ppermute(block, axis, route)


def with_neighbours(block, axis, dim):
    count = lax.axis_size(axis)
    before = lax.ppermute(block, axis, [(i, i + 1) for i in range(count - 1)])
    after = lax.ppermute(block, axis, [(i + 1, i) for i in range(count - 1)])
    return jnp.concatenate([before, block, after], axis=dim)


def pad_grid(field):
    widths = [(0, 0)] * (field.ndim - 2) + [(1, 1), (1, 1)]
    return jnp.pad(field, widths)


def laplace(padded, center):
    return (
        padded[..., 2:, 1:-1]
        + padded[..., :-2, 1:-1]
        + padded[..., 1:-1, 2:]
        + padded[..., 1:-1, :-2]
        - 4.0 * center
    )


def forward_rate(state, speed_x, speed_y, damping, source, mask):
    padded = pad_grid(state)
    grad_x = 0.5 * (padded[..., 2:, 1:-1] - padded[..., :-2, 1:-1])
    grad_y = 0.5 * (padded[..., 1:-1, 2:] - padded[..., 1:-1, :-2])
    rate = source - (speed_x * grad_x + speed_y * grad_y) + DIFFUSE * laplace(padded, state) - damping * state
    return rate * mask


def adjoint_rate(state, speed_x, speed_y, damping, source, mask):
    padded = pad_grid(state)
    flux_x = pad_grid(speed_x * state)
    flux_y = pad_grid(speed_y * state)
    div_x = 0.5 * (flux_x[..., 2:, 1:-1] - flux_x[..., :-2, 1:-1])
    div_y = 0.5 * (flux_y[..., 1:-1, 2:] - flux_y[..., 1:-1, :-2])
    rate = source + div_x + div_y + DIFFUSE * laplace(padded, state) - damping * state
    return rate * mask


def coefficient_table(chosen, phase, periods):
    turns = chosen[:, None] * phase[None, :] % periods
    angle = 2.0 * math.pi / periods * turns.astype(jnp.float32)
    table = jnp.stack([jnp.cos(angle), -jnp.sin(angle)], axis=1) * (1.0 / math.sqrt(periods))
    return table.reshape(2 * chosen.shape[0], phase.shape[0])


def on_device(base_flow, forcing, damping, harmonics):
    steps = forcing.shape[0]
    count_f, rows, columns = (forcing.shape[1], forcing.shape[2], forcing.shape[3])
    slabs = lax.axis_size("slab")
    tiles = lax.axis_size("tile")
    periods = steps * slabs

    packed = jnp.concatenate(
        [base_flow.reshape(2 * steps, rows, columns), forcing.reshape(steps * count_f, rows, columns), damping[None]],
        axis=0,
    )

    def band(depth):
        return min(rows, -(-depth // 8) * 8)

    def cut(field, have, want):
        return lax.slice_in_dim(field, have - want, have + rows + want, axis=field.ndim - 2)

    tail = 2 * steps
    fwd_need = [0] * steps
    fwd_need[-1] = 2 * steps - 1
    for m in range(steps - 2, -1, -1):
        fwd_need[m] = max(2 * m + 1, fwd_need[m + 1] + 2)
    fwd_need = [max(need, 2 * m + 2) for m, need in enumerate(fwd_need)]
    far = band(fwd_need[0])
    assert far <= rows

    before = lax.ppermute(packed[:, rows - far :], "tile", [(i, i + 1) for i in range(tiles - 1)])
    after = lax.ppermute(packed[:, :far], "tile", [(i + 1, i) for i in range(tiles - 1)])
    wide = jnp.concatenate([before, packed, after], axis=1)

    def fields(block, have):
        ext = rows + 2 * have
        flow = block[: 2 * steps].reshape(2, steps, ext, columns)
        drive = block[2 * steps : 2 * steps + steps * count_f].reshape(steps, count_f, ext, columns)
        row = lax.axis_index("tile") * rows - have + jnp.arange(ext, dtype=jnp.int32)
        mask = ((row >= 0) & (row < tiles * rows)).astype(jnp.float32)[:, None]
        return flow, drive, block[-1], mask, have

    sweep_fields = [fields(wide, far)] * 2
    def slab_start(own, shift, depth):
        onward = lambda j, t: ((j + shift) % slabs) * tiles + t
        both = ("slab", "tile")
        up = lax.ppermute(own[:, rows - depth :], both,
                          [(j * tiles + t, onward(j, t + 1)) for j in range(slabs) for t in range(tiles - 1)])
        down = lax.ppermute(own[:, :depth], both,
                            [(j * tiles + t + 1, onward(j, t)) for j in range(slabs) for t in range(tiles - 1)])
        return jnp.concatenate([up, passed_along(own, "slab", shift), down], axis=1)

    sweep_bands = [
        [band(2 * (steps - m)) for m in range(steps)],
        [band(need) for need in fwd_need],
    ]

    have = sweep_bands[0][0]
    start = jnp.zeros((count_f, rows + 2 * have, columns), jnp.float32)
    for sweep in range(SWEEPS):
        flow, drive, damp, mask, held = sweep_fields[min(sweep, 1)]
        state = start
        record = []
        for step in range(steps):
            want = sweep_bands[min(sweep, 1)][step]
            state = cut(state, have, want)
            have = want
            record.append((state, have))
            speed_x = cut(flow[0, step], held, want)
            speed_y = cut(flow[1, step], held, want)
            damp_here, mask_here = cut(damp, held, want), cut(mask, held, want)
            source = cut(drive[step], held, want)
            first = forward_rate(state, speed_x, speed_y, damp_here, source, mask_here)
            second = forward_rate(state + first, speed_x, speed_y, damp_here, source, mask_here)
            state = state + 0.5 * (first + second)
        if sweep + 1 < SWEEPS:
            start = slab_start(cut(state, have, 0), 1, far)
            have = far
    response = record
    adj_bands = [
        [band(2 * m + 2) for m in range(steps)],
        [band(2 * m + 2) for m in range(steps)],
    ]
    flow, drive, damp, mask, held = sweep_fields[1]
    have = adj_bands[0][steps - 1]
    start = jnp.zeros((count_f, rows + 2 * have, columns), jnp.float32)
    for sweep in range(SWEEPS):
        state = start
        record = [None] * steps
        for step in range(steps - 1, -1, -1):
            want = adj_bands[min(sweep, 1)][step]
            state = cut(state, have, want)
            have = want
            speed_x = cut(flow[0, step], held, want)
            speed_y = cut(flow[1, step], held, want)
            damp_here, mask_here = cut(damp, held, want), cut(mask, held, want)
            source = cut(response[step][0], response[step][1], want)
            first = adjoint_rate(state, speed_x, speed_y, damp_here, source, mask_here)
            second = adjoint_rate(state + first, speed_x, speed_y, damp_here, source, mask_here)
            state = state + 0.5 * (first + second)
            record[step] = cut(state, have, 0)
        if sweep + 1 < SWEEPS:
            start = slab_start(cut(state, have, 0), -1, tail)
            have = tail
    phase = lax.axis_index("slab") * steps + jnp.arange(steps, dtype=jnp.int32)
    table = coefficient_table(harmonics, phase, periods)
    terms = sum(table[:, m, None, None, None] * record[m][None] for m in range(steps))
    parts = lax.all_to_all(terms.reshape(slabs, 2 * H // slabs, count_f, rows, columns), "slab", 0, 0, tiled=True)
    return jnp.sum(parts, axis=0, keepdims=True)


def solution(mesh):
    return jax.shard_map(
        on_device,
        mesh=mesh,
        in_specs=(
            P(None, "slab", "tile", None),
            P("slab", None, "tile", None),
            P("tile", None),
            P(),
        ),
        out_specs=P("slab", None, None, "tile", None),
        check_vma=False,
    )
```

```python
import math

import jax
import jax.numpy as jnp
from jax import lax
from jax.sharding import PartitionSpec as P

SWEEPS = 2
H = 8


DIFFUSE = 0.15


def passed_along(block, axis, distance):
    devices = range(lax.axis_size(axis))
    route = [((i - distance) % len(devices), i) for i in devices]
    return lax.ppermute(block, axis, route)


def with_neighbours(block, axis, dim):
    count = lax.axis_size(axis)
    before = lax.ppermute(block, axis, [(i, i + 1) for i in range(count - 1)])
    after = lax.ppermute(block, axis, [(i + 1, i) for i in range(count - 1)])
    return jnp.concatenate([before, block, after], axis=dim)


def pad_grid(field):
    widths = [(0, 0)] * (field.ndim - 2) + [(1, 1), (1, 1)]
    return jnp.pad(field, widths)


def laplace(padded, center):
    return (
        padded[..., 2:, 1:-1]
        + padded[..., :-2, 1:-1]
        + padded[..., 1:-1, 2:]
        + padded[..., 1:-1, :-2]
        - 4.0 * center
    )


def forward_rate(state, speed_x, speed_y, damping, source, mask):
    padded = pad_grid(state)
    grad_x = 0.5 * (padded[..., 2:, 1:-1] - padded[..., :-2, 1:-1])
    grad_y = 0.5 * (padded[..., 1:-1, 2:] - padded[..., 1:-1, :-2])
    rate = source - (speed_x * grad_x + speed_y * grad_y) + DIFFUSE * laplace(padded, state) - damping * state
    return rate * mask


def adjoint_rate(state, speed_x, speed_y, damping, source, mask):
    padded = pad_grid(state)
    flux_x = pad_grid(speed_x * state)
    flux_y = pad_grid(speed_y * state)
    div_x = 0.5 * (flux_x[..., 2:, 1:-1] - flux_x[..., :-2, 1:-1])
    div_y = 0.5 * (flux_y[..., 1:-1, 2:] - flux_y[..., 1:-1, :-2])
    rate = source + div_x + div_y + DIFFUSE * laplace(padded, state) - damping * state
    return rate * mask


def coefficient_table(chosen, phase, periods):
    turns = chosen[:, None] * phase[None, :] % periods
    angle = 2.0 * math.pi / periods * turns.astype(jnp.float32)
    table = jnp.stack([jnp.cos(angle), -jnp.sin(angle)], axis=1) * (1.0 / math.sqrt(periods))
    return table.reshape(2 * chosen.shape[0], phase.shape[0])


def on_device(base_flow, forcing, damping, harmonics):
    steps = forcing.shape[0]
    count_f, rows, columns = (forcing.shape[1], forcing.shape[2], forcing.shape[3])
    slabs = lax.axis_size("slab")
    tiles = lax.axis_size("tile")
    periods = steps * slabs

    packed = jnp.concatenate(
        [base_flow.reshape(2 * steps, rows, columns), forcing.reshape(steps * count_f, rows, columns), damping[None]],
        axis=0,
    )

    def band(depth):
        return min(rows, -(-depth // 8) * 8)

    def cut(field, have, want):
        return lax.slice_in_dim(field, have - want, have + rows + want, axis=field.ndim - 2)

    tail = 2 * steps
    fwd_need = [2 * (steps - 1 - m) for m in range(steps)]
    reach = [band(2 * m + 1) for m in range(steps)]
    far = max(band(fwd_need[0] + 2), band(2 * steps))
    assert far <= rows

    before = lax.ppermute(packed[:, rows - far :], "tile", [(i, i + 1) for i in range(tiles - 1)])
    after = lax.ppermute(packed[:, :far], "tile", [(i + 1, i) for i in range(tiles - 1)])
    wide = jnp.concatenate([before, packed, after], axis=1)

    def fields(block, have):
        ext = rows + 2 * have
        flow = block[: 2 * steps].reshape(2, steps, ext, columns)
        drive = block[2 * steps : 2 * steps + steps * count_f].reshape(steps, count_f, ext, columns)
        row = lax.axis_index("tile") * rows - have + jnp.arange(ext, dtype=jnp.int32)
        mask = ((row >= 0) & (row < tiles * rows)).astype(jnp.float32)[:, None]
        return flow, drive, block[-1], mask, have

    sweep_fields = [fields(wide, far)] * 2
    def slab_start(own, shift, depth):
        onward = lambda j, t: ((j + shift) % slabs) * tiles + t
        both = ("slab", "tile")
        up = lax.ppermute(own[:, rows - depth :], both,
                          [(j * tiles + t, onward(j, t + 1)) for j in range(slabs) for t in range(tiles - 1)])
        down = lax.ppermute(own[:, :depth], both,
                            [(j * tiles + t + 1, onward(j, t)) for j in range(slabs) for t in range(tiles - 1)])
        return jnp.concatenate([up, passed_along(own, "slab", shift), down], axis=1)

    sweep_bands = [
        [band(2 * (steps - m)) for m in range(steps)],
        [band(need) for need in fwd_need],
    ]

    have = sweep_bands[0][0]
    start = jnp.zeros((count_f, rows + 2 * have, columns), jnp.float32)
    for sweep in range(SWEEPS):
        flow, drive, damp, mask, held = sweep_fields[min(sweep, 1)]
        state = start
        record = []
        for step in range(steps):
            want = sweep_bands[min(sweep, 1)][step]
            state = cut(state, have, want)
            have = want
            record.append((state, have))
            speed_x = cut(flow[0, step], held, want)
            speed_y = cut(flow[1, step], held, want)
            damp_here, mask_here = cut(damp, held, want), cut(mask, held, want)
            source = cut(drive[step], held, want)
            first = forward_rate(state, speed_x, speed_y, damp_here, source, mask_here)
            second = forward_rate(state + first, speed_x, speed_y, damp_here, source, mask_here)
            state = state + 0.5 * (first + second)
        if sweep + 1 < SWEEPS:
            start = slab_start(cut(state, have, 0), 1, far)
            have = far
    centre = [cut(state_m, held_m, 0) for state_m, held_m in record]
    down = jnp.concatenate([q[:, rows - d :].reshape(-1, columns) for q, d in zip(centre, reach)], axis=0)
    up = jnp.concatenate([q[:, :d].reshape(-1, columns) for q, d in zip(centre, reach)], axis=0)
    from_before = lax.ppermute(down, "tile", [(i, i + 1) for i in range(tiles - 1)])
    from_after = lax.ppermute(up, "tile", [(i + 1, i) for i in range(tiles - 1)])
    response, at = [], 0
    for q, d in zip(centre, reach):
        size = count_f * d
        head = from_before[at : at + size].reshape(count_f, d, columns)
        foot = from_after[at : at + size].reshape(count_f, d, columns)
        response.append((jnp.concatenate([head, q, foot], axis=1), d))
        at += size
    adj_bands = [
        [band(2 * m + 2) for m in range(steps)],
        [band(2 * m + 2) for m in range(steps)],
    ]
    flow, drive, damp, mask, held = sweep_fields[1]
    have = adj_bands[0][steps - 1]
    start = jnp.zeros((count_f, rows + 2 * have, columns), jnp.float32)
    for sweep in range(SWEEPS):
        state = start
        record = [None] * steps
        for step in range(steps - 1, -1, -1):
            want = adj_bands[min(sweep, 1)][step]
            state = cut(state, have, want)
            have = want
            speed_x = cut(flow[0, step], held, want)
            speed_y = cut(flow[1, step], held, want)
            damp_here, mask_here = cut(damp, held, want), cut(mask, held, want)
            source = cut(response[step][0], response[step][1], want)
            first = adjoint_rate(state, speed_x, speed_y, damp_here, source, mask_here)
            second = adjoint_rate(state + first, speed_x, speed_y, damp_here, source, mask_here)
            state = state + 0.5 * (first + second)
            record[step] = cut(state, have, 0)
        if sweep + 1 < SWEEPS:
            start = slab_start(cut(state, have, 0), -1, tail)
            have = tail
    adjoint = jnp.stack(record, axis=0)
    phase = lax.axis_index("slab") * steps + jnp.arange(steps, dtype=jnp.int32)
    flat = adjoint.reshape(steps, count_f * rows * columns)
    table = coefficient_table(harmonics, phase, periods)
    terms = jnp.dot(table, flat, precision=lax.Precision.HIGHEST)
    parts = lax.all_to_all(terms.reshape(slabs, 2 * H // slabs, count_f, rows, columns), "slab", 0, 0, tiled=True)
    return jnp.sum(parts, axis=0, keepdims=True)


def solution(mesh):
    return jax.shard_map(
        on_device,
        mesh=mesh,
        in_specs=(
            P(None, "slab", "tile", None),
            P("slab", None, "tile", None),
            P("tile", None),
            P(),
        ),
        out_specs=P("slab", None, None, "tile", None),
        check_vma=False,
    )
```

```python
import math

import jax
import jax.numpy as jnp
from jax import lax
from jax.sharding import PartitionSpec as P

SWEEPS = 2
H = 8


DIFFUSE = 0.15


def passed_along(block, axis, distance):
    devices = range(lax.axis_size(axis))
    route = [((i - distance) % len(devices), i) for i in devices]
    return lax.ppermute(block, axis, route)


def with_neighbours(block, axis, dim):
    count = lax.axis_size(axis)
    before = lax.ppermute(block, axis, [(i, i + 1) for i in range(count - 1)])
    after = lax.ppermute(block, axis, [(i + 1, i) for i in range(count - 1)])
    return jnp.concatenate([before, block, after], axis=dim)


def pad_grid(field):
    widths = [(0, 0)] * (field.ndim - 2) + [(1, 1), (1, 1)]
    return jnp.pad(field, widths)


def laplace(padded, center):
    return (
        padded[..., 2:, 1:-1]
        + padded[..., :-2, 1:-1]
        + padded[..., 1:-1, 2:]
        + padded[..., 1:-1, :-2]
        - 4.0 * center
    )


def forward_rate(state, speed_x, speed_y, damping, source, mask):
    padded = pad_grid(state)
    grad_x = 0.5 * (padded[..., 2:, 1:-1] - padded[..., :-2, 1:-1])
    grad_y = 0.5 * (padded[..., 1:-1, 2:] - padded[..., 1:-1, :-2])
    rate = source - (speed_x * grad_x + speed_y * grad_y) + DIFFUSE * laplace(padded, state) - damping * state
    return rate * mask


def adjoint_rate(state, speed_x, speed_y, damping, source, mask):
    padded = pad_grid(state)
    flux_x = pad_grid(speed_x * state)
    flux_y = pad_grid(speed_y * state)
    div_x = 0.5 * (flux_x[..., 2:, 1:-1] - flux_x[..., :-2, 1:-1])
    div_y = 0.5 * (flux_y[..., 1:-1, 2:] - flux_y[..., 1:-1, :-2])
    rate = source + div_x + div_y + DIFFUSE * laplace(padded, state) - damping * state
    return rate * mask


def coefficient_table(chosen, phase, periods):
    turns = chosen[:, None] * phase[None, :] % periods
    angle = 2.0 * math.pi / periods * turns.astype(jnp.float32)
    table = jnp.stack([jnp.cos(angle), -jnp.sin(angle)], axis=1) * (1.0 / math.sqrt(periods))
    return table.reshape(2 * chosen.shape[0], phase.shape[0])


def on_device(base_flow, forcing, damping, harmonics):
    steps = forcing.shape[0]
    count_f, rows, columns = (forcing.shape[1], forcing.shape[2], forcing.shape[3])
    slabs = lax.axis_size("slab")
    tiles = lax.axis_size("tile")
    periods = steps * slabs

    packed = jnp.concatenate(
        [base_flow.reshape(2 * steps, rows, columns), forcing.reshape(steps * count_f, rows, columns), damping[None]],
        axis=0,
    )

    def band(depth):
        return min(rows, -(-depth // 8) * 8)

    def cut(field, have, want):
        return lax.slice_in_dim(field, have - want, have + rows + want, axis=field.ndim - 2)

    tail = 2 * steps
    fwd_need = [0] * steps
    fwd_need[-1] = 2 * steps - 1
    for m in range(steps - 2, -1, -1):
        fwd_need[m] = max(2 * m + 1, fwd_need[m + 1] + 2)
    fwd_need = [max(need, 2 * m + 2) for m, need in enumerate(fwd_need)]
    far = band(fwd_need[0])
    assert far <= rows

    near = band(2 * steps)
    tile_down = [(i, i + 1) for i in range(tiles - 1)]
    tile_up = [(i + 1, i) for i in range(tiles - 1)]
    before = lax.ppermute(packed[:, rows - near :], "tile", tile_down)
    after = lax.ppermute(packed[:, :near], "tile", tile_up)
    (far_down, far_up), (before, after) = lax.optimization_barrier(
        ((packed[:, rows - far : rows - near], packed[:, near:far]), (before, after))
    )
    before_far = lax.ppermute(far_down, "tile", tile_down)
    after_far = lax.ppermute(far_up, "tile", tile_up)
    narrow = jnp.concatenate([before, packed, after], axis=1)
    wide = jnp.concatenate([before_far, before, packed, after, after_far], axis=1)

    def fields(block, have):
        ext = rows + 2 * have
        flow = block[: 2 * steps].reshape(2, steps, ext, columns)
        drive = block[2 * steps : 2 * steps + steps * count_f].reshape(steps, count_f, ext, columns)
        row = lax.axis_index("tile") * rows - have + jnp.arange(ext, dtype=jnp.int32)
        mask = ((row >= 0) & (row < tiles * rows)).astype(jnp.float32)[:, None]
        return flow, drive, block[-1], mask, have

    sweep_fields = [fields(narrow, near), fields(wide, far)]
    def slab_start(own, shift, depth):
        onward = lambda j, t: ((j + shift) % slabs) * tiles + t
        both = ("slab", "tile")
        up = lax.ppermute(own[:, rows - depth :], both,
                          [(j * tiles + t, onward(j, t + 1)) for j in range(slabs) for t in range(tiles - 1)])
        down = lax.ppermute(own[:, :depth], both,
                            [(j * tiles + t + 1, onward(j, t)) for j in range(slabs) for t in range(tiles - 1)])
        return jnp.concatenate([up, passed_along(own, "slab", shift), down], axis=1)

    sweep_bands = [
        [band(2 * (steps - m)) for m in range(steps)],
        [band(need) for need in fwd_need],
    ]

    have = sweep_bands[0][0]
    start = jnp.zeros((count_f, rows + 2 * have, columns), jnp.float32)
    for sweep in range(SWEEPS):
        flow, drive, damp, mask, held = sweep_fields[min(sweep, 1)]
        state = start
        record = []
        for step in range(steps):
            want = sweep_bands[min(sweep, 1)][step]
            state = cut(state, have, want)
            have = want
            record.append((state, have))
            speed_x = cut(flow[0, step], held, want)
            speed_y = cut(flow[1, step], held, want)
            damp_here, mask_here = cut(damp, held, want), cut(mask, held, want)
            source = cut(drive[step], held, want)
            first = forward_rate(state, speed_x, speed_y, damp_here, source, mask_here)
            second = forward_rate(state + first, speed_x, speed_y, damp_here, source, mask_here)
            state = state + 0.5 * (first + second)
        if sweep + 1 < SWEEPS:
            start = slab_start(cut(state, have, 0), 1, far)
            have = far
    response = record
    adj_bands = [
        [band(2 * m + 2) for m in range(steps)],
        [band(2 * m + 2) for m in range(steps)],
    ]
    flow, drive, damp, mask, held = sweep_fields[0]
    have = adj_bands[0][steps - 1]
    start = jnp.zeros((count_f, rows + 2 * have, columns), jnp.float32)
    for sweep in range(SWEEPS):
        state = start
        record = [None] * steps
        for step in range(steps - 1, -1, -1):
            want = adj_bands[min(sweep, 1)][step]
            state = cut(state, have, want)
            have = want
            speed_x = cut(flow[0, step], held, want)
            speed_y = cut(flow[1, step], held, want)
            damp_here, mask_here = cut(damp, held, want), cut(mask, held, want)
            source = cut(response[step][0], response[step][1], want)
            first = adjoint_rate(state, speed_x, speed_y, damp_here, source, mask_here)
            second = adjoint_rate(state + first, speed_x, speed_y, damp_here, source, mask_here)
            state = state + 0.5 * (first + second)
            record[step] = cut(state, have, 0)
        if sweep + 1 < SWEEPS:
            start = slab_start(cut(state, have, 0), -1, tail)
            have = tail
    adjoint = jnp.stack(record, axis=0)
    phase = lax.axis_index("slab") * steps + jnp.arange(steps, dtype=jnp.int32)
    flat = adjoint.reshape(steps, count_f * rows * columns)
    table = coefficient_table(harmonics, phase, periods)
    terms = jnp.dot(table, flat, precision=lax.Precision.HIGHEST)
    parts = lax.all_to_all(terms.reshape(slabs, 2 * H // slabs, count_f, rows, columns), "slab", 0, 0, tiled=True)
    return jnp.sum(parts, axis=0, keepdims=True)


def solution(mesh):
    return jax.shard_map(
        on_device,
        mesh=mesh,
        in_specs=(
            P(None, "slab", "tile", None),
            P("slab", None, "tile", None),
            P("tile", None),
            P(),
        ),
        out_specs=P("slab", None, None, "tile", None),
        check_vma=False,
    )
```

```python
import math

import jax
import jax.numpy as jnp
from jax import lax
from jax.sharding import PartitionSpec as P


SWEEPS = 2
H = 8


DIFFUSE = 0.15


def passed_along(block, axis, distance):
    devices = range(lax.axis_size(axis))
    route = [((i - distance) % len(devices), i) for i in devices]
    return lax.ppermute(block, axis, route)


def pad_grid(field):
    widths = [(0, 0)] * (field.ndim - 2) + [(1, 1), (1, 1)]
    return jnp.pad(field, widths)


def laplace(padded, center):
    return (
        padded[..., 2:, 1:-1]
        + padded[..., :-2, 1:-1]
        + padded[..., 1:-1, 2:]
        + padded[..., 1:-1, :-2]
        - 4.0 * center
    )


def forward_rate(state, speed_x, speed_y, damping, source, mask):
    padded = pad_grid(state)
    grad_x = 0.5 * (padded[..., 2:, 1:-1] - padded[..., :-2, 1:-1])
    grad_y = 0.5 * (padded[..., 1:-1, 2:] - padded[..., 1:-1, :-2])
    rate = source - (speed_x * grad_x + speed_y * grad_y) + DIFFUSE * laplace(padded, state) - damping * state
    return rate * mask


def adjoint_rate(state, speed_x, speed_y, damping, source, mask):
    padded = pad_grid(state)
    flux_x = pad_grid(speed_x * state)
    flux_y = pad_grid(speed_y * state)
    div_x = 0.5 * (flux_x[..., 2:, 1:-1] - flux_x[..., :-2, 1:-1])
    div_y = 0.5 * (flux_y[..., 1:-1, 2:] - flux_y[..., 1:-1, :-2])
    rate = source + div_x + div_y + DIFFUSE * laplace(padded, state) - damping * state
    return rate * mask


def coefficient_table(chosen, phase, periods):
    turns = chosen[:, None] * phase[None, :] % periods
    angle = 2.0 * math.pi / periods * turns.astype(jnp.float32)
    table = jnp.stack([jnp.cos(angle), -jnp.sin(angle)], axis=1) * (1.0 / math.sqrt(periods))
    return table.reshape(2 * chosen.shape[0], phase.shape[0])


def whole(base_flow, forcing, damping, harmonics):
    steps = forcing.shape[0]
    count_f, rows, columns = (forcing.shape[1], forcing.shape[2], forcing.shape[3])
    slabs = lax.axis_size("slab")
    tiles = lax.axis_size("tile")
    periods = steps * slabs

    packed = jnp.concatenate(
        [base_flow.reshape(2 * steps, rows, columns), forcing.reshape(steps * count_f, rows, columns), damping[None]],
        axis=0,
    )

    def band(depth):
        return min(rows, -(-depth // 8) * 8)

    def cut(field, have, want):
        return lax.slice_in_dim(field, have - want, have + rows + want, axis=field.ndim - 2)

    tail = 2 * steps
    fwd_need = [0] * steps
    fwd_need[-1] = 2 * steps - 1
    for m in range(steps - 2, -1, -1):
        fwd_need[m] = max(2 * m + 1, fwd_need[m + 1] + 2)
    fwd_need = [max(need, 2 * m + 2) for m, need in enumerate(fwd_need)]
    far = band(fwd_need[0])
    assert far <= rows

    near = band(2 * steps)
    tile_down = [(i, i + 1) for i in range(tiles - 1)]
    tile_up = [(i + 1, i) for i in range(tiles - 1)]
    before = lax.ppermute(packed[:, rows - near :], "tile", tile_down)
    after = lax.ppermute(packed[:, :near], "tile", tile_up)
    (far_down, far_up), (before, after) = lax.optimization_barrier(
        ((packed[:, rows - far : rows - near], packed[:, near:far]), (before, after))
    )
    before_far = lax.ppermute(far_down, "tile", tile_down)
    after_far = lax.ppermute(far_up, "tile", tile_up)
    narrow = jnp.concatenate([before, packed, after], axis=1)
    wide = jnp.concatenate([before_far, before, packed, after, after_far], axis=1)

    def fields(block, have):
        ext = rows + 2 * have
        flow = block[: 2 * steps].reshape(2, steps, ext, columns)
        drive = block[2 * steps : 2 * steps + steps * count_f].reshape(steps, count_f, ext, columns)
        row = lax.axis_index("tile") * rows - have + jnp.arange(ext, dtype=jnp.int32)
        mask = ((row >= 0) & (row < tiles * rows)).astype(jnp.float32)[:, None]
        return flow, drive, block[-1], mask, have

    sweep_fields = [fields(narrow, near), fields(wide, far)]

    def slab_start(own, shift, depth):
        onward = lambda j, t: ((j + shift) % slabs) * tiles + t
        both = ("slab", "tile")
        up = lax.ppermute(own[:, rows - depth :], both,
                          [(j * tiles + t, onward(j, t + 1)) for j in range(slabs) for t in range(tiles - 1)])
        down = lax.ppermute(own[:, :depth], both,
                            [(j * tiles + t + 1, onward(j, t)) for j in range(slabs) for t in range(tiles - 1)])
        return jnp.concatenate([up, passed_along(own, "slab", shift), down], axis=1)

    sweep_bands = [
        [band(2 * (steps - m)) for m in range(steps)],
        [band(need) for need in fwd_need],
    ]

    have = sweep_bands[0][0]
    start = jnp.zeros((count_f, rows + 2 * have, columns), jnp.float32)
    for sweep in range(SWEEPS):
        flow, drive, damp, mask, held = sweep_fields[min(sweep, 1)]
        state = start
        record = []
        for step in range(steps):
            want = sweep_bands[min(sweep, 1)][step]
            state = cut(state, have, want)
            have = want
            record.append((state, have))
            speed_x = cut(flow[0, step], held, want)
            speed_y = cut(flow[1, step], held, want)
            damp_here, mask_here = cut(damp, held, want), cut(mask, held, want)
            source = cut(drive[step], held, want)
            first = forward_rate(state, speed_x, speed_y, damp_here, source, mask_here)
            second = forward_rate(state + first, speed_x, speed_y, damp_here, source, mask_here)
            state = state + 0.5 * (first + second)
        if sweep + 1 < SWEEPS:
            start = slab_start(cut(state, have, 0), 1, far)
            have = far
    response = record
    adj_bands = [
        [band(2 * m + 2) for m in range(steps)],
        [band(2 * m + 2) for m in range(steps)],
    ]
    flow, drive, damp, mask, held = sweep_fields[0]
    have = adj_bands[0][steps - 1]
    start = jnp.zeros((count_f, rows + 2 * have, columns), jnp.float32)
    for sweep in range(SWEEPS):
        state = start
        record = [None] * steps
        for step in range(steps - 1, -1, -1):
            want = adj_bands[min(sweep, 1)][step]
            state = cut(state, have, want)
            have = want
            speed_x = cut(flow[0, step], held, want)
            speed_y = cut(flow[1, step], held, want)
            damp_here, mask_here = cut(damp, held, want), cut(mask, held, want)
            source = cut(response[step][0], response[step][1], want)
            first = adjoint_rate(state, speed_x, speed_y, damp_here, source, mask_here)
            second = adjoint_rate(state + first, speed_x, speed_y, damp_here, source, mask_here)
            state = state + 0.5 * (first + second)
            record[step] = cut(state, have, 0)
        if sweep + 1 < SWEEPS:
            start = slab_start(cut(state, have, 0), -1, tail)
            have = tail
    phase = lax.axis_index("slab") * steps + jnp.arange(steps, dtype=jnp.int32)
    table = coefficient_table(harmonics, phase, periods)
    terms = sum(table[:, m, None, None, None] * record[m][None] for m in range(steps))
    parts = lax.all_to_all(terms.reshape(slabs, 2 * H // slabs, count_f, rows, columns), "slab", 0, 0, tiled=True)
    return jnp.sum(parts, axis=0, keepdims=True)


def solution(mesh):
    return jax.shard_map(
        whole,
        mesh=mesh,
        in_specs=(
            P(None, "slab", "tile", None),
            P("slab", None, "tile", None),
            P("tile", None),
            P(),
        ),
        out_specs=P("slab", None, None, "tile", None),
        check_vma=False,
    )
```

```python
import math

import jax
import jax.numpy as jnp
from jax import lax
from jax.sharding import PartitionSpec as P


SWEEPS = 2
H = 8


DIFFUSE = 0.15


def passed_along(block, axis, distance):
    devices = range(lax.axis_size(axis))
    route = [((i - distance) % len(devices), i) for i in devices]
    return lax.ppermute(block, axis, route)


def pad_grid(field):
    widths = [(0, 0)] * (field.ndim - 2) + [(1, 1), (1, 1)]
    return jnp.pad(field, widths)


def laplace(padded, center):
    return (
        padded[..., 2:, 1:-1]
        + padded[..., :-2, 1:-1]
        + padded[..., 1:-1, 2:]
        + padded[..., 1:-1, :-2]
        - 4.0 * center
    )


def forward_rate(state, speed_x, speed_y, damping, source, mask):
    padded = pad_grid(state)
    grad_x = 0.5 * (padded[..., 2:, 1:-1] - padded[..., :-2, 1:-1])
    grad_y = 0.5 * (padded[..., 1:-1, 2:] - padded[..., 1:-1, :-2])
    rate = source - (speed_x * grad_x + speed_y * grad_y) + DIFFUSE * laplace(padded, state) - damping * state
    return rate * mask


def adjoint_rate(state, speed_x, speed_y, damping, source, mask):
    padded = pad_grid(state)
    flux_x = pad_grid(speed_x * state)
    flux_y = pad_grid(speed_y * state)
    div_x = 0.5 * (flux_x[..., 2:, 1:-1] - flux_x[..., :-2, 1:-1])
    div_y = 0.5 * (flux_y[..., 1:-1, 2:] - flux_y[..., 1:-1, :-2])
    rate = source + div_x + div_y + DIFFUSE * laplace(padded, state) - damping * state
    return rate * mask


def coefficient_table(chosen, phase, periods):
    turns = chosen[:, None] * phase[None, :] % periods
    angle = 2.0 * math.pi / periods * turns.astype(jnp.float32)
    table = jnp.stack([jnp.cos(angle), -jnp.sin(angle)], axis=1) * (1.0 / math.sqrt(periods))
    return table.reshape(2 * chosen.shape[0], phase.shape[0])


def whole(base_flow, forcing, damping, harmonics):
    steps = forcing.shape[0]
    count_f, rows, columns = (forcing.shape[1], forcing.shape[2], forcing.shape[3])
    slabs = lax.axis_size("slab")
    tiles = lax.axis_size("tile")
    periods = steps * slabs

    packed = jnp.concatenate(
        [base_flow.reshape(2 * steps, rows, columns), forcing.reshape(steps * count_f, rows, columns), damping[None]],
        axis=0,
    )

    def band(depth):
        return min(rows, -(-depth // 8) * 8)

    def cut(field, have, want):
        return lax.slice_in_dim(field, have - want, have + rows + want, axis=field.ndim - 2)

    tail = 2 * steps
    fwd_need = [0] * steps
    fwd_need[-1] = 2 * steps - 1
    for m in range(steps - 2, -1, -1):
        fwd_need[m] = max(2 * m + 1, fwd_need[m + 1] + 2)
    fwd_need = [max(need, 2 * m + 2) for m, need in enumerate(fwd_need)]
    far = band(fwd_need[0])
    assert far <= rows

    near = band(2 * steps)
    tile_down = [(i, i + 1) for i in range(tiles - 1)]
    tile_up = [(i + 1, i) for i in range(tiles - 1)]

    def rows_of(lo, hi):
        return jnp.concatenate(
            [
                base_flow[:, :, lo:hi].reshape(2 * steps, hi - lo, columns),
                forcing[:, :, lo:hi].reshape(steps * count_f, hi - lo, columns),
                damping[None, lo:hi],
            ],
            axis=0,
        )

    before = lax.ppermute(rows_of(rows - near, rows), "tile", tile_down)
    after = lax.ppermute(rows_of(0, near), "tile", tile_up)
    (far_down, far_up), (before, after) = lax.optimization_barrier(
        ((rows_of(rows - far, rows - near), rows_of(near, far)), (before, after))
    )
    before_far = lax.ppermute(far_down, "tile", tile_down)
    after_far = lax.ppermute(far_up, "tile", tile_up)
    narrow = jnp.concatenate([before, packed, after], axis=1)
    wide = jnp.concatenate([before_far, before, packed, after, after_far], axis=1)

    def fields(block, have):
        ext = rows + 2 * have
        flow = block[: 2 * steps].reshape(2, steps, ext, columns)
        drive = block[2 * steps : 2 * steps + steps * count_f].reshape(steps, count_f, ext, columns)
        row = lax.axis_index("tile") * rows - have + jnp.arange(ext, dtype=jnp.int32)
        mask = ((row >= 0) & (row < tiles * rows)).astype(jnp.float32)[:, None]
        return flow, drive, block[-1], mask, have

    sweep_fields = [fields(narrow, near), fields(wide, far)]

    def slab_start(own, shift, depth):
        onward = lambda j, t: ((j + shift) % slabs) * tiles + t
        both = ("slab", "tile")
        up = lax.ppermute(own[:, rows - depth :], both,
                          [(j * tiles + t, onward(j, t + 1)) for j in range(slabs) for t in range(tiles - 1)])
        down = lax.ppermute(own[:, :depth], both,
                            [(j * tiles + t + 1, onward(j, t)) for j in range(slabs) for t in range(tiles - 1)])
        return jnp.concatenate([up, passed_along(own, "slab", shift), down], axis=1)

    sweep_bands = [
        [band(2 * (steps - m)) for m in range(steps)],
        [band(need) for need in fwd_need],
    ]

    have = sweep_bands[0][0]
    start = jnp.zeros((count_f, rows + 2 * have, columns), jnp.float32)
    for sweep in range(SWEEPS):
        flow, drive, damp, mask, held = sweep_fields[min(sweep, 1)]
        state = start
        record = []
        for step in range(steps):
            want = sweep_bands[min(sweep, 1)][step]
            state = cut(state, have, want)
            have = want
            record.append((state, have))
            speed_x = cut(flow[0, step], held, want)
            speed_y = cut(flow[1, step], held, want)
            damp_here, mask_here = cut(damp, held, want), cut(mask, held, want)
            source = cut(drive[step], held, want)
            first = forward_rate(state, speed_x, speed_y, damp_here, source, mask_here)
            second = forward_rate(state + first, speed_x, speed_y, damp_here, source, mask_here)
            state = state + 0.5 * (first + second)
        if sweep + 1 < SWEEPS:
            start = slab_start(cut(state, have, 0), 1, far)
            have = far
    response = record
    adj_bands = [
        [band(2 * m + 2) for m in range(steps)],
        [band(2 * m + 2) for m in range(steps)],
    ]
    flow, drive, damp, mask, held = sweep_fields[0]
    have = adj_bands[0][steps - 1]
    start = jnp.zeros((count_f, rows + 2 * have, columns), jnp.float32)
    for sweep in range(SWEEPS):
        state = start
        record = [None] * steps
        for step in range(steps - 1, -1, -1):
            want = adj_bands[min(sweep, 1)][step]
            state = cut(state, have, want)
            have = want
            speed_x = cut(flow[0, step], held, want)
            speed_y = cut(flow[1, step], held, want)
            damp_here, mask_here = cut(damp, held, want), cut(mask, held, want)
            source = cut(response[step][0], response[step][1], want)
            first = adjoint_rate(state, speed_x, speed_y, damp_here, source, mask_here)
            second = adjoint_rate(state + first, speed_x, speed_y, damp_here, source, mask_here)
            state = state + 0.5 * (first + second)
            record[step] = cut(state, have, 0)
        if sweep + 1 < SWEEPS:
            start = slab_start(cut(state, have, 0), -1, tail)
            have = tail
    phase = lax.axis_index("slab") * steps + jnp.arange(steps, dtype=jnp.int32)
    table = coefficient_table(harmonics, phase, periods)
    terms = sum(table[:, m, None, None, None] * record[m][None] for m in range(steps))
    parts = lax.all_to_all(terms.reshape(slabs, 2 * H // slabs, count_f, rows, columns), "slab", 0, 0, tiled=True)
    return jnp.sum(parts, axis=0, keepdims=True)


def solution(mesh):
    return jax.shard_map(
        whole,
        mesh=mesh,
        in_specs=(
            P(None, "slab", "tile", None),
            P("slab", None, "tile", None),
            P("tile", None),
            P(),
        ),
        out_specs=P("slab", None, None, "tile", None),
        check_vma=False,
    )
```
